512 devices in a mesh: dp: 16 (over z, core), expert: 32 (over x, y).
Axes of the slice: x: 4, y: 8, z: 8, core: 2. Of those that a mesh axis runs over, the one named last changes fastest.
Arguments:
- tokens: bfloat16 [65536, 1024], P(('dp', 'expert')), may hold values from -6 to 6
- expert_ids: int32 [65536, 8], P(('dp', 'expert')), may hold values from 0 to 63, all different within a row; in each aligned block of 128 rows (0 to 127, 128 to 255, ...) at most 17 rows name the same one
- gate_values: float32 [65536, 8], P(('dp', 'expert')), may hold values from 0.05 to 0.5
- w_gate: bfloat16 [64, 1024, 384], P('expert', 'dp'), may hold values from -0.1875 to 0.1875
- w_up: bfloat16 [64, 1024, 384], P('expert', 'dp'), may hold values from -0.1875 to 0.1875
- w_down: bfloat16 [64, 384, 1024], P('expert', 'dp'), may hold values from -0.3125 to 0.3125
- partner: int32 [512], replicated, may hold values from 0 to 511, as said below
Outputs:
- contrast_loss: float32 [], replicated
- token_grad: bfloat16 [65536, 1024], P(('dp', 'expert'))
- gate_grad: float32 [65536, 8], P(('dp', 'expert'))
The draws below stay inside these ranges and needn't reach their ends.
Inputs may be any that keep to these rules, and one draw needn't show every extreme that they name: `expert_ids`: each row names 8 different experts. Among the 128 rows of one sequence no expert is named more than 17 times, and in every draw some sequence names some expert exactly 17 times. partner[i] differs from i.
All inputs are finite; a program needn't handle non-finite values.
Results may differ from the reference program's by a relative error of at most 0.014.
Values may be sent and summed in bfloat16 or wider, within the bound.
No kernel may reach another device: no remote copies, remote signals or barrier semaphores. Data moves between devices by JAX's collectives and lax.ppermute only.
A program may use at most 64 MiB of HBM per device.

```python
import math
import jax
import jax.numpy as jnp
import numpy as np
from jax import lax

D = 1024
FF = 384
TOPK = 8
TOK_DEV = 128
EXPERTS = 64
CAP = 17
BATCH = 512
TOKENS = 65536


def draw_partner(key, part):
    offset = jax.random.randint(key, (BATCH,), 1, BATCH, dtype=jnp.int32)
    return ((jnp.arange(BATCH, dtype=jnp.int32) + offset) % BATCH).astype(jnp.int32)


def steps_of(own_key, shape, cuts, low, largest):
    loudness = 1.0
    for dim, blocks in cuts:
        steps = jax.random.uniform(jax.random.fold_in(jax.random.fold_in(own_key, 6), dim), (blocks,), jnp.float32, low / len(cuts), largest / len(cuts))
        loudness = loudness * jnp.repeat(jnp.exp(steps), shape[dim] // blocks).reshape((-1,) + (1,) * (len(shape) - 1 - dim))
    return loudness


def shared_out(key, own, number, rows, amount, top, bound, lean):
    sequence = jax.random.permutation(key, amount)
    heavy_load, usual = shares(amount, rows * top, bound, lean, True), shares(amount, rows * top, bound, lean, False)
    places = jnp.arange(amount)

    def named(lengths, rotation):
        used = int((lengths > 0).sum())
        fixed = max(1, used // 4)
        moved = fixed + (places - fixed + rotation * (used - fixed)) % max(1, amount - fixed)
        return jnp.zeros((amount,), jnp.int32).at[sequence[jnp.where(places < fixed, places, moved)]].set(jnp.asarray(lengths, jnp.int32))

    lengths = jnp.where(number % 4 == 0, named(heavy_load, number // 4), named(usual, number - number // 4 - 1))
    mixed = jax.random.permutation(jax.random.fold_in(own, 3), amount)
    giver, taker = mixed[0:amount // 2 * 2:2], mixed[1:amount // 2 * 2:2]
    margin = jnp.minimum(lengths[giver] - 1, bound - lengths[taker]) // 2
    margin = jnp.where((giver == sequence[0]) | (taker == sequence[0]) | (lengths[taker] == 0), 0, jnp.maximum(margin, 0))
    moved = jax.random.randint(jax.random.fold_in(own, 4), (amount // 2,), 0, 1 << 20) % (margin + 1)
    lengths = lengths.at[giver].add(-moved).at[taker].add(moved)
    labels = jnp.searchsorted(jnp.cumsum(lengths), jnp.arange(rows * top), side="right").astype(jnp.int32)
    table = labels.reshape(top, rows).T
    table = table[jax.random.permutation(jax.random.fold_in(own, 1), rows)]
    rotation = jax.random.randint(jax.random.fold_in(own, 2), (rows, 1), 0, top)
    return jnp.take_along_axis(table, (jnp.arange(top)[None, :] + rotation) % top, axis=1)


def shares(number_of, total, bound, skew, full):
    weights = [(1 << 20) // math.isqrt(grade ** skew) + 1 for grade in range(1, number_of + 1)]
    largest = bound if full else min(bound, max(-(-total // number_of), total * weights[0] // sum(weights)))
    least = 1 if total - largest >= number_of - 1 else 0
    holding, surplus = [largest] + [least] * (number_of - 1), total - largest - least * (number_of - 1)
    while surplus > 0:
        candidates = [i for i in range(1, number_of) if holding[i] < largest] or [i for i in range(1, number_of) if holding[i] < bound]
        pool, budget = sum([weights[i] for i in candidates]), surplus
        for i in candidates:
            extra = min(bound - holding[i], max(1, budget * weights[i] // pool), surplus)
            holding[i] = holding[i] + extra
            surplus = surplus - extra
    return np.array(holding)


def gaussian(rng, extent, scale, most, pieces=(), held_as=jnp.bfloat16):
    gain = steps_of(rng, extent, pieces, -0.22, 0.18) if pieces else 1.0
    result = jax.random.normal(rng, extent, jnp.float32) * scale * gain
    return jnp.minimum(jnp.maximum(result, -most), most).astype(held_as)


def setup_inputs(seed: int = 0) -> dict:
    key_list = jax.random.split(jax.random.key(seed), 8)
    tokens = gaussian(key_list[0], (TOKENS, D), 1.0, 6.0, ((0, 512),))
    expert_ids_keys = jax.random.split(jax.random.fold_in(key_list[1], 1), TOKENS // TOK_DEV)
    expert_ids_turns = jax.random.permutation(jax.random.fold_in(key_list[1], 3), TOKENS // TOK_DEV)
    expert_ids = jax.vmap(lambda own, number: shared_out(jax.random.fold_in(key_list[1], 2), own, number, TOK_DEV, EXPERTS, TOPK, CAP, 2))(expert_ids_keys, expert_ids_turns).reshape((TOKENS, TOPK))
    gate_values = jnp.clip(jnp.exp(math.log(0.5) - 2.3025851 * jax.random.uniform(key_list[2], (TOKENS, TOPK), jnp.float32) ** steps_of(key_list[2], (TOKENS, TOPK), ((0, 512),), -0.2, 0.2)), 0.05, 0.5)
    w_gate = gaussian(key_list[3], (EXPERTS, D, FF), D ** -0.5, 0.1875, ((0, 32), (1, 16)))
    w_up = gaussian(key_list[4], (EXPERTS, D, FF), D ** -0.5, 0.1875, ((0, 32), (1, 16)))
    w_down = gaussian(key_list[5], (EXPERTS, FF, D), FF ** -0.5, 0.3125, ((0, 32), (1, 16)))
    partner = draw_partner(jax.random.fold_in(key_list[7], 71), 0)
    return dict(tokens=tokens, expert_ids=expert_ids, gate_values=gate_values, w_gate=w_gate, w_up=w_up, w_down=w_down, partner=partner)


score_scale = 20.0
highest = lax.Precision.HIGHEST

def silu_parts(pre_act):
    sigmoid_val = jax.nn.sigmoid(pre_act)
    return (pre_act * sigmoid_val, sigmoid_val * (1.0 + pre_act * (1.0 - sigmoid_val)))

def expert_forward(rows_in, gate_one, up_one, down_one):
    pre_gate = jnp.dot(rows_in, gate_one, preferred_element_type=jnp.float32)
    pre_up = jnp.dot(rows_in, up_one, preferred_element_type=jnp.float32)
    activated, derivative = silu_parts(pre_gate)
    hidden = (activated * pre_up).astype(jnp.bfloat16)
    expert_out = jnp.dot(hidden, down_one, preferred_element_type=jnp.float32).astype(jnp.bfloat16)
    return (pre_gate, pre_up, activated, derivative, expert_out)

def reference(tokens, expert_ids, gate_values, w_gate, w_up, w_down, partner):
    route_ids = expert_ids.reshape(BATCH, TOK_DEV, TOPK)
    gate_rows = gate_values.reshape(BATCH, TOK_DEV, TOPK)
    expert_iota = jnp.arange(EXPERTS, dtype=jnp.int32)
    chosen = lax.optimization_barrier(jnp.sum((route_ids[:, :, :, None] == expert_iota).astype(jnp.int32), axis=2, dtype=jnp.int32))
    before = (jnp.cumsum(chosen, axis=1, dtype=jnp.int32) - chosen).astype(jnp.int32)
    slot_rank = jnp.take_along_axis(before, route_ids, axis=2).astype(jnp.int32)
    grid_shape = (BATCH, TOK_DEV, TOPK)
    seq_index = jnp.broadcast_to(jnp.arange(BATCH, dtype=jnp.int32)[:, None, None], grid_shape)
    tok_index = jnp.broadcast_to(jnp.arange(TOK_DEV, dtype=jnp.int32)[None, :, None], grid_shape)
    route_index = jnp.broadcast_to(jnp.arange(TOPK, dtype=jnp.int32)[None, None, :], grid_shape)
    slot_tok = jnp.full((BATCH, EXPERTS, CAP), TOK_DEV, jnp.int32).at[seq_index, route_ids, slot_rank].set(tok_index)
    slot_gate = jnp.zeros((BATCH, EXPERTS, CAP), jnp.float32).at[seq_index, route_ids, slot_rank].set(gate_rows)
    slot_route = jnp.zeros((BATCH, EXPERTS, CAP), jnp.int32).at[seq_index, route_ids, slot_rank].set(route_index)
    padded = jnp.concatenate([tokens.reshape(BATCH, TOK_DEV, D), jnp.zeros((BATCH, 1, D), tokens.dtype)], axis=1)
    seq_column = jnp.arange(BATCH, dtype=jnp.int32)[:, None]
    expert_range = jnp.arange(EXPERTS, dtype=jnp.int32)

    def expert_inputs(expert_pos):
        slot_rows = slot_tok[:, expert_pos]
        rows_in = padded[seq_column, slot_rows].reshape(BATCH * CAP, D)
        return (slot_rows, rows_in, w_gate[expert_pos], w_up[expert_pos], w_down[expert_pos])

    def forward_step(mixed_sum, expert_pos):
        slot_rows, rows_in, gate_one, up_one, down_one = expert_inputs(expert_pos)
        expert_out = expert_forward(rows_in, gate_one, up_one, down_one)[4]
        scaled = slot_gate[:, expert_pos][:, :, None] * expert_out.astype(jnp.float32).reshape(BATCH, CAP, D)
        return (mixed_sum.at[seq_column, slot_rows].add(scaled), None)
    mixed_sum, ignored = lax.scan(forward_step, jnp.zeros((BATCH, TOK_DEV + 1, D), jnp.float32), expert_range)
    mixed_rows = tokens.reshape(BATCH, TOK_DEV, D).astype(jnp.float32) + mixed_sum[:, :TOK_DEV]
    pooled = lax.optimization_barrier(jnp.mean(mixed_rows, axis=1))
    inv_rms = lax.rsqrt(lax.optimization_barrier(jnp.mean(pooled * pooled, axis=1)) + 1e-06)
    embedding = (pooled * inv_rms[:, None]).astype(jnp.bfloat16)
    all_embed = embedding.astype(jnp.float32)
    scores = score_scale / D * jnp.dot(all_embed, all_embed.T, precision=highest)
    batch_iota = jnp.arange(BATCH, dtype=jnp.int32)
    others = batch_iota[:, None] != batch_iota[None, :]
    log_total = jnp.log(lax.optimization_barrier(jnp.sum(jnp.where(others, jnp.exp(scores), 0.0), axis=1)))
    partner_score = jnp.take_along_axis(scores, partner[:, None].astype(jnp.int32), axis=1)[:, 0]
    contrast_loss = jnp.mean(log_total - partner_score)
    partner_hit = (batch_iota[None, :] == partner[:, None]).astype(jnp.float32)
    weight = jnp.where(others, jnp.exp(scores - log_total[:, None]), 0.0) - partner_hit
    embed_grad = score_scale / D * (jnp.dot(weight, all_embed, precision=highest) + jnp.dot(weight.T, all_embed, precision=highest))
    seq_grad = inv_rms[:, None] * embed_grad - (inv_rms ** 3 * lax.optimization_barrier(jnp.sum(pooled * embed_grad, axis=1)) / D)[:, None] * pooled

    def backward_step(carry, expert_pos):
        grad_sum, gate_sum = carry
        slot_rows, rows_in, gate_one, up_one, down_one = expert_inputs(expert_pos)
        pre_gate, pre_up, activated, derivative, expert_out = expert_forward(rows_in, gate_one, up_one, down_one)
        out_rows = expert_out.astype(jnp.float32).reshape(BATCH, CAP, D)
        gate_part = lax.optimization_barrier(jnp.sum(out_rows * seq_grad[:, None, :], axis=2))
        gate_sum = gate_sum.at[seq_column, slot_rows, slot_route[:, expert_pos]].add(gate_part)
        out_grad = (slot_gate[:, expert_pos][:, :, None] * seq_grad[:, None, :]).astype(jnp.bfloat16).reshape(BATCH * CAP, D)
        hidden_grad = jnp.dot(out_grad, down_one.T, preferred_element_type=jnp.float32)
        gate_side = (hidden_grad * pre_up * derivative).astype(jnp.bfloat16)
        up_side = (hidden_grad * activated).astype(jnp.bfloat16)
        route_grad = (jnp.dot(gate_side, gate_one.T, preferred_element_type=jnp.float32) + jnp.dot(up_side, up_one.T, preferred_element_type=jnp.float32)).astype(jnp.bfloat16)
        grad_sum = grad_sum.at[seq_column, slot_rows].add(route_grad.astype(jnp.float32).reshape(BATCH, CAP, D))
        return ((grad_sum, gate_sum), None)
    start = (jnp.zeros((BATCH, TOK_DEV + 1, D), jnp.float32), jnp.zeros((BATCH, TOK_DEV + 1, TOPK), jnp.float32))
    (grad_sum, gate_sum), ignored = lax.scan(backward_step, start, expert_range)
    token_grad = (seq_grad[:, None, :] + grad_sum[:, :TOK_DEV]).astype(jnp.bfloat16).reshape(TOKENS, D)
    gate_grad = gate_sum[:, :TOK_DEV].reshape(TOKENS, TOPK)
    return (contrast_loss, token_grad, gate_grad)
```

```python
import jax
import jax.numpy as jnp
from jax import lax
from jax.sharding import PartitionSpec as P

score_scale = 20.0
highest = lax.Precision.HIGHEST
f32 = jnp.float32
bf16 = jnp.bfloat16


def silu_parts(pre_act):
    sigmoid_val = jax.nn.sigmoid(pre_act)
    return (pre_act * sigmoid_val, sigmoid_val * (1.0 + pre_act * (1.0 - sigmoid_val)))


def split3(x):
    hi = lax.reduce_precision(x, exponent_bits=8, mantissa_bits=7)
    rest = x - hi
    mid = lax.reduce_precision(rest, exponent_bits=8, mantissa_bits=7)
    lo = rest - mid
    return jnp.concatenate([hi, mid, lo], axis=-1).astype(bf16)


def join3(packed, n):
    hi = packed[..., :n].astype(f32)
    mid = packed[..., n : 2 * n].astype(f32)
    lo = packed[..., 2 * n : 3 * n].astype(f32)
    return hi + (mid + lo)


def pack_row(values, width):
    pieces = split3(values)
    pad = width - pieces.shape[-1]
    pieces = jnp.pad(pieces, [(0, 0)] * (pieces.ndim - 1) + [(0, pad)])
    return pieces[..., None, :]


def on_device(tokens, expert_ids, gate_values, w_gate, w_up, w_down, partner):
    tok_rows, model_width = tokens.shape
    route_count = expert_ids.shape[1]
    local_experts = w_gate.shape[0]
    group = lax.axis_size("expert")
    experts = group * local_experts
    capacity = tok_rows * route_count // experts + max(1, tok_rows * route_count // (16 * experts))
    slot_total = experts * capacity
    me = lax.axis_index("expert")
    row_block = lax.axis_index("dp")

    gate_full, up_full, down_full = (
        lax.all_gather(w_gate, "dp", axis=1, tiled=True),
        lax.all_gather(w_up, "dp", axis=1, tiled=True),
        lax.all_gather(w_down, "dp", axis=1, tiled=True),
    )

    expert_iota = jnp.arange(experts, dtype=jnp.int32)
    matches = expert_ids[:, :, None] == expert_iota
    chosen = jnp.sum(matches.astype(jnp.int32), axis=1, dtype=jnp.int32)
    chosen_gate = jnp.sum(jnp.where(matches, gate_values[:, :, None], 0.0), axis=1)
    before = jnp.cumsum(chosen, axis=0, dtype=jnp.int32) - chosen
    slot_rank = jnp.take_along_axis(before, expert_ids, axis=1)
    slot_row = (expert_ids * capacity + slot_rank).reshape(-1)
    slot_iota = jnp.arange(capacity, dtype=jnp.int32)
    onehot = (chosen.T[:, None, :] == 1) & (before.T[:, None, :] == slot_iota[None, :, None])
    placer = onehot.astype(bf16)
    slot_gate = jnp.sum(jnp.where(onehot, chosen_gate.T[:, None, :], 0.0), axis=2)
    outgoing = jnp.einsum("ect,td->ecd", placer, tokens, preferred_element_type=f32).astype(bf16)
    outgoing = jnp.concatenate([outgoing, pack_row(slot_gate, model_width)], axis=1)
    outgoing = outgoing.reshape(experts, 1, capacity + 1, model_width)
    placer_flat = placer.reshape(slot_total, tok_rows)

    arrived = lax.all_to_all(outgoing, "expert", split_axis=0, concat_axis=1, tiled=True)
    rows_in = arrived[:, :, :capacity, :]
    gates = join3(arrived[:, :, capacity, :], capacity)
    pre_gate = jnp.einsum("escd,edf->escf", rows_in, gate_full, preferred_element_type=f32)
    pre_up = jnp.einsum("escd,edf->escf", rows_in, up_full, preferred_element_type=f32)
    activated, derivative = silu_parts(pre_gate)
    hidden = (activated * pre_up).astype(bf16)
    expert_out = jnp.einsum("escf,efd->escd", hidden, down_full, preferred_element_type=f32).astype(
        bf16
    )
    out_f32 = expert_out.astype(f32)
    partial = jnp.sum(gates[..., None] * out_f32, axis=(0, 2))

    token_mean = jnp.mean(tokens.astype(f32), axis=0)
    own_row = (jnp.arange(group, dtype=jnp.int32) == me)[:, None]
    share = partial / tok_rows + jnp.where(own_row, token_mean[None, :], 0.0)
    pooled = lax.psum(share, "expert")
    inv_rms = lax.rsqrt(jnp.mean(pooled * pooled, axis=1) + 1e-06)
    embedding = (pooled * inv_rms[:, None]).astype(bf16)
    gathered = lax.all_gather(embedding, "dp", axis=0, tiled=True)
    batch_size = gathered.shape[0]

    scores = (
        score_scale
        / model_width
        * lax.dot_general(
            gathered, gathered, (((1,), (1,)), ((), ())), preferred_element_type=f32
        )
    )
    batch_iota = jnp.arange(batch_size, dtype=jnp.int32)
    others = batch_iota[:, None] != batch_iota[None, :]
    log_total = jnp.log(jnp.sum(jnp.where(others, jnp.exp(scores), 0.0), axis=1))
    partner_score = jnp.take_along_axis(scores, partner[:, None], axis=1)[:, 0]
    contrast_loss = jnp.mean(log_total - partner_score)

    first = row_block * group
    rows = first + jnp.arange(group, dtype=jnp.int32)
    row_scores = lax.dynamic_slice_in_dim(scores, first, group, axis=0)
    row_totals = lax.dynamic_slice_in_dim(log_total, first, group, axis=0)
    row_partner = lax.dynamic_slice_in_dim(partner, first, group, axis=0)
    row_others = rows[:, None] != batch_iota[None, :]
    row_weight = jnp.where(row_others, jnp.exp(row_scores - row_totals[:, None]), 0.0) - (
        batch_iota[None, :] == row_partner[:, None]
    ).astype(f32)
    col_scores = lax.dynamic_slice_in_dim(scores, first, group, axis=1).T
    col_weight = jnp.where(row_others, jnp.exp(col_scores - log_total[None, :]), 0.0) - (
        rows[:, None] == partner[None, :]
    ).astype(f32)
    embed_grad = (
        score_scale
        / model_width
        * jnp.dot(row_weight + col_weight, gathered.astype(f32), precision=highest)
    )
    seq_grad = (
        inv_rms[:, None] * embed_grad
        - (inv_rms**3 * jnp.sum(pooled * embed_grad, axis=1) / model_width)[:, None] * pooled
    )

    slot_dots = jnp.sum(out_f32 * seq_grad[None, :, None, :], axis=3)
    out_grad = (gates[..., None] * seq_grad[None, :, None, :]).astype(bf16)
    hidden_grad = jnp.einsum("escd,efd->escf", out_grad, down_full, preferred_element_type=f32)
    gate_side = (hidden_grad * pre_up * derivative).astype(bf16)
    up_side = (hidden_grad * activated).astype(bf16)
    route_here = jnp.einsum("escf,edf->escd", gate_side, gate_full, preferred_element_type=f32)
    route_here = (
        route_here
        + jnp.einsum("escf,edf->escd", up_side, up_full, preferred_element_type=f32)
    ).astype(bf16)
    route_here = jnp.concatenate([route_here, pack_row(slot_dots, model_width)], axis=2)
    returned = lax.all_to_all(route_here, "expert", split_axis=1, concat_axis=0, tiled=True)
    returned = returned.reshape(experts, capacity + 1, model_width)

    route_rows = returned[:, :capacity, :].reshape(slot_total, model_width)
    slot_grads = join3(returned[:, capacity, :], capacity).reshape(slot_total)
    gate_grad = jnp.take(slot_grads, slot_row, axis=0).reshape(tok_rows, route_count)
    route_sum = jnp.einsum("st,sd->td", placer_flat, route_rows, preferred_element_type=f32)
    own_grad = lax.dynamic_index_in_dim(seq_grad, me, axis=0, keepdims=False)
    token_grad = (own_grad[None, :] + route_sum).astype(bf16)
    return (contrast_loss, token_grad, gate_grad)


def solution(mesh):
    placed = (
        P(("dp", "expert"), None),
        P(("dp", "expert"), None),
        P(("dp", "expert"), None),
        P("expert", "dp", None),
        P("expert", "dp", None),
        P("expert", "dp", None),
        P(),
    )
    return jax.shard_map(
        on_device,
        mesh=mesh,
        in_specs=placed,
        out_specs=(P(), P(("dp", "expert"), None), P(("dp", "expert"), None)),
        check_vma=False,
    )
```

```python
import jax
import jax.numpy as jnp
from jax import lax
from jax.sharding import PartitionSpec as P

score_scale = 20.0
highest = lax.Precision.HIGHEST
f32 = jnp.float32
bf16 = jnp.bfloat16


def silu_parts(pre_act):
    sigmoid_val = jax.nn.sigmoid(pre_act)
    return (pre_act * sigmoid_val, sigmoid_val * (1.0 + pre_act * (1.0 - sigmoid_val)))


def split3(x):
    hi = lax.reduce_precision(x, exponent_bits=8, mantissa_bits=7)
    rest = x - hi
    mid = lax.reduce_precision(rest, exponent_bits=8, mantissa_bits=7)
    lo = rest - mid
    return jnp.concatenate([hi, mid, lo], axis=-1).astype(bf16)


def join3(packed, n):
    hi = packed[..., :n].astype(f32)
    mid = packed[..., n : 2 * n].astype(f32)
    lo = packed[..., 2 * n : 3 * n].astype(f32)
    return hi + (mid + lo)


def pack_row(values, width):
    pieces = split3(values)
    pad = width - pieces.shape[-1]
    pieces = jnp.pad(pieces, [(0, 0)] * (pieces.ndim - 1) + [(0, pad)])
    return pieces[..., None, :]


def on_device(tokens, expert_ids, gate_values, w_gate, w_up, w_down, partner):
    tok_rows, model_width = tokens.shape
    route_count = expert_ids.shape[1]
    local_experts = w_gate.shape[0]
    group = lax.axis_size("expert")
    experts = group * local_experts
    capacity = tok_rows * route_count // experts + max(1, tok_rows * route_count // (16 * experts))
    slot_total = experts * capacity
    me = lax.axis_index("expert")
    row_block = lax.axis_index("dp")

    ff_width = w_gate.shape[2]
    stacked = jnp.stack([w_gate, w_up, w_down.reshape(w_gate.shape)])
    every = lax.all_gather(stacked, "dp", axis=0, tiled=False)
    parts = every.shape[0]

    def joined(k, slab, inner):
        return jnp.swapaxes(every[:, k].reshape((parts, local_experts) + slab), 0, 1).reshape(
            (local_experts, parts * slab[0]) + inner
        )

    gate_full = joined(0, w_gate.shape[1:], (ff_width,))
    up_full = joined(1, w_gate.shape[1:], (ff_width,))
    down_full = joined(2, w_down.shape[1:], (model_width,))

    expert_iota = jnp.arange(experts, dtype=jnp.int32)
    matches = expert_ids[:, :, None] == expert_iota
    chosen = jnp.sum(matches.astype(jnp.int32), axis=1, dtype=jnp.int32)
    chosen_gate = jnp.sum(jnp.where(matches, gate_values[:, :, None], 0.0), axis=1)
    before = jnp.cumsum(chosen, axis=0, dtype=jnp.int32) - chosen
    slot_rank = jnp.take_along_axis(before, expert_ids, axis=1)
    slot_row = (expert_ids * capacity + slot_rank).reshape(-1)
    slot_iota = jnp.arange(capacity, dtype=jnp.int32)
    onehot = (chosen.T[:, None, :] == 1) & (before.T[:, None, :] == slot_iota[None, :, None])
    placer = onehot.astype(bf16)
    slot_gate = jnp.sum(jnp.where(onehot, chosen_gate.T[:, None, :], 0.0), axis=2)
    outgoing = jnp.einsum("ect,td->ecd", placer, tokens, preferred_element_type=f32).astype(bf16)
    outgoing = jnp.concatenate([outgoing, pack_row(slot_gate, model_width)], axis=1)
    outgoing = outgoing.reshape(experts, 1, capacity + 1, model_width)
    placer_flat = placer.reshape(slot_total, tok_rows)

    arrived = lax.all_to_all(outgoing, "expert", split_axis=0, concat_axis=1, tiled=True)
    rows_in = arrived[:, :, :capacity, :]
    gates = join3(arrived[:, :, capacity, :], capacity)
    pre_gate = jnp.einsum("escd,edf->escf", rows_in, gate_full, preferred_element_type=f32)
    pre_up = jnp.einsum("escd,edf->escf", rows_in, up_full, preferred_element_type=f32)
    activated, derivative = silu_parts(pre_gate)
    hidden = (activated * pre_up).astype(bf16)
    expert_out = jnp.einsum("escf,efd->escd", hidden, down_full, preferred_element_type=f32).astype(
        bf16
    )
    out_f32 = expert_out.astype(f32)
    partial = jnp.sum(gates[..., None] * out_f32, axis=(0, 2))

    token_mean = jnp.mean(tokens.astype(f32), axis=0)
    shares = lax.all_to_all(partial / tok_rows, "expert", split_axis=0, concat_axis=0, tiled=True)
    own_pooled = token_mean + jnp.sum(shares, axis=0)
    copies = jnp.broadcast_to(own_pooled[None, :], (group, model_width))
    pooled = lax.all_to_all(copies, "expert", split_axis=0, concat_axis=0, tiled=True)
    inv_rms = lax.rsqrt(jnp.mean(pooled * pooled, axis=1) + 1e-06)
    embedding = (pooled * inv_rms[:, None]).astype(bf16)
    gathered = lax.all_gather(embedding, "dp", axis=0, tiled=True)
    batch_size = gathered.shape[0]

    scores = (
        score_scale
        / model_width
        * lax.dot_general(
            gathered, gathered, (((1,), (1,)), ((), ())), preferred_element_type=f32
        )
    )
    batch_iota = jnp.arange(batch_size, dtype=jnp.int32)
    others = batch_iota[:, None] != batch_iota[None, :]
    log_total = jnp.log(jnp.sum(jnp.where(others, jnp.exp(scores), 0.0), axis=1))
    partner_score = jnp.take_along_axis(scores, partner[:, None], axis=1)[:, 0]
    contrast_loss = jnp.mean(log_total - partner_score)

    first = row_block * group
    rows = first + jnp.arange(group, dtype=jnp.int32)
    row_scores = lax.dynamic_slice_in_dim(scores, first, group, axis=0)
    row_totals = lax.dynamic_slice_in_dim(log_total, first, group, axis=0)
    row_partner = lax.dynamic_slice_in_dim(partner, first, group, axis=0)
    row_others = rows[:, None] != batch_iota[None, :]
    row_weight = jnp.where(row_others, jnp.exp(row_scores - row_totals[:, None]), 0.0) - (
        batch_iota[None, :] == row_partner[:, None]
    ).astype(f32)
    col_scores = lax.dynamic_slice_in_dim(scores, first, group, axis=1).T
    col_weight = jnp.where(row_others, jnp.exp(col_scores - log_total[None, :]), 0.0) - (
        rows[:, None] == partner[None, :]
    ).astype(f32)
    embed_grad = (
        score_scale
        / model_width
        * jnp.dot(row_weight + col_weight, gathered.astype(f32), precision=highest)
    )
    seq_grad = (
        inv_rms[:, None] * embed_grad
        - (inv_rms**3 * jnp.sum(pooled * embed_grad, axis=1) / model_width)[:, None] * pooled
    )

    slot_dots = jnp.sum(out_f32 * seq_grad[None, :, None, :], axis=3)
    out_grad = (gates[..., None] * seq_grad[None, :, None, :]).astype(bf16)
    hidden_grad = jnp.einsum("escd,efd->escf", out_grad, down_full, preferred_element_type=f32)
    gate_side = (hidden_grad * pre_up * derivative).astype(bf16)
    up_side = (hidden_grad * activated).astype(bf16)
    route_here = jnp.einsum("escf,edf->escd", gate_side, gate_full, preferred_element_type=f32)
    route_here = (
        route_here
        + jnp.einsum("escf,edf->escd", up_side, up_full, preferred_element_type=f32)
    ).astype(bf16)
    route_here = jnp.concatenate([route_here, pack_row(slot_dots, model_width)], axis=2)
    returned = lax.all_to_all(route_here, "expert", split_axis=1, concat_axis=0, tiled=True)
    returned = returned.reshape(experts, capacity + 1, model_width)

    route_rows = returned[:, :capacity, :].reshape(slot_total, model_width)
    slot_grads = join3(returned[:, capacity, :], capacity).reshape(slot_total)
    gate_grad = jnp.take(slot_grads, slot_row, axis=0).reshape(tok_rows, route_count)
    route_sum = jnp.einsum("st,sd->td", placer_flat, route_rows, preferred_element_type=f32)
    own_grad = lax.dynamic_index_in_dim(seq_grad, me, axis=0, keepdims=False)
    token_grad = (own_grad[None, :] + route_sum).astype(bf16)
    return (contrast_loss, token_grad, gate_grad)


def solution(mesh):
    placed = (
        P(("dp", "expert"), None),
        P(("dp", "expert"), None),
        P(("dp", "expert"), None),
        P("expert", "dp", None),
        P("expert", "dp", None),
        P("expert", "dp", None),
        P(),
    )
    return jax.shard_map(
        on_device,
        mesh=mesh,
        in_specs=placed,
        out_specs=(P(), P(("dp", "expert"), None), P(("dp", "expert"), None)),
        check_vma=False,
    )
```

```python
import jax
import jax.numpy as jnp
from jax import lax
from jax.sharding import PartitionSpec as P

score_scale = 20.0
highest = lax.Precision.HIGHEST
f32 = jnp.float32
bf16 = jnp.bfloat16


def silu_parts(pre_act):
    sigmoid_val = jax.nn.sigmoid(pre_act)
    return (pre_act * sigmoid_val, sigmoid_val * (1.0 + pre_act * (1.0 - sigmoid_val)))


def split3(x):
    hi = lax.reduce_precision(x, exponent_bits=8, mantissa_bits=7)
    rest = x - hi
    mid = lax.reduce_precision(rest, exponent_bits=8, mantissa_bits=7)
    lo = rest - mid
    return jnp.concatenate([hi, mid, lo], axis=-1).astype(bf16)


def join3(packed, n):
    hi = packed[..., :n].astype(f32)
    mid = packed[..., n : 2 * n].astype(f32)
    lo = packed[..., 2 * n : 3 * n].astype(f32)
    return hi + (mid + lo)


def pack_row(values, width):
    pieces = split3(values)
    pad = width - pieces.shape[-1]
    pieces = jnp.pad(pieces, [(0, 0)] * (pieces.ndim - 1) + [(0, pad)])
    return pieces[..., None, :]


def on_device(tokens, expert_ids, gate_values, w_gate, w_up, w_down, partner):
    tok_rows, model_width = tokens.shape
    route_count = expert_ids.shape[1]
    local_experts = w_gate.shape[0]
    group = lax.axis_size("expert")
    experts = group * local_experts
    capacity = tok_rows * route_count // experts + max(1, tok_rows * route_count // (16 * experts))
    slot_total = experts * capacity
    me = lax.axis_index("expert")
    row_block = lax.axis_index("dp")

    ff_width = w_gate.shape[2]
    stacked = jnp.stack([w_gate, w_up, w_down.reshape(w_gate.shape)])
    every = lax.all_gather(stacked, "dp", axis=2, tiled=True)
    gate_full = every[0]
    up_full = every[1]
    down_full = every[2].reshape(local_experts, ff_width, model_width)

    expert_iota = jnp.arange(experts, dtype=jnp.int32)
    matches = expert_ids[:, :, None] == expert_iota
    chosen = jnp.sum(matches.astype(jnp.int32), axis=1, dtype=jnp.int32)
    chosen_gate = jnp.sum(jnp.where(matches, gate_values[:, :, None], 0.0), axis=1)
    before = jnp.cumsum(chosen, axis=0, dtype=jnp.int32) - chosen
    slot_rank = jnp.sum(jnp.where(matches, before[:, None, :], 0), axis=2, dtype=jnp.int32)
    slot_iota = jnp.arange(capacity, dtype=jnp.int32)
    onehot = (chosen.T[:, None, :] == 1) & (before.T[:, None, :] == slot_iota[None, :, None])
    placer = onehot.astype(bf16)
    slot_gate = jnp.sum(jnp.where(onehot, chosen_gate.T[:, None, :], 0.0), axis=2)
    outgoing = jnp.einsum("ect,td->ecd", placer, tokens, preferred_element_type=f32).astype(bf16)
    outgoing = jnp.concatenate([outgoing, pack_row(slot_gate, model_width)], axis=1)
    outgoing = outgoing.reshape(group, local_experts, capacity + 1, model_width)
    placer_flat = placer.reshape(slot_total, tok_rows)

    arrived = lax.all_to_all(outgoing, "expert", split_axis=0, concat_axis=0, tiled=True)
    rows_in = arrived[:, :, :capacity, :]
    gates = join3(arrived[:, :, capacity, :], capacity)
    pre_gate = jnp.einsum("secd,edf->secf", rows_in, gate_full, preferred_element_type=f32)
    pre_up = jnp.einsum("secd,edf->secf", rows_in, up_full, preferred_element_type=f32)
    activated, derivative = silu_parts(pre_gate)
    hidden = (activated * pre_up).astype(bf16)
    expert_out = jnp.einsum("secf,efd->secd", hidden, down_full, preferred_element_type=f32).astype(
        bf16
    )
    out_f32 = expert_out.astype(f32)
    partial = jnp.sum(gates[..., None] * out_f32, axis=(1, 2))

    token_mean = jnp.mean(tokens.astype(f32), axis=0)
    shares = lax.all_to_all(partial / tok_rows, "expert", split_axis=0, concat_axis=0, tiled=True)
    own_pooled = token_mean + jnp.sum(shares, axis=0)
    copies = jnp.broadcast_to(own_pooled[None, :], (group, model_width))
    pooled = lax.all_to_all(copies, "expert", split_axis=0, concat_axis=0, tiled=True)
    inv_rms = lax.rsqrt(jnp.mean(pooled * pooled, axis=1) + 1e-06)
    embedding = (pooled * inv_rms[:, None]).astype(bf16)
    blocks = lax.axis_size("dp")
    spread = jnp.broadcast_to(embedding[None], (blocks, group, model_width))
    gathered = lax.all_to_all(spread, "dp", split_axis=0, concat_axis=0, tiled=True)
    gathered = gathered.reshape(blocks * group, model_width)
    batch_size = gathered.shape[0]

    scores = (
        score_scale
        / model_width
        * lax.dot_general(
            gathered, gathered, (((1,), (1,)), ((), ())), preferred_element_type=f32
        )
    )
    batch_iota = jnp.arange(batch_size, dtype=jnp.int32)
    others = batch_iota[:, None] != batch_iota[None, :]
    log_total = jnp.log(jnp.sum(jnp.where(others, jnp.exp(scores), 0.0), axis=1))
    partner_hit = batch_iota[None, :] == partner[:, None]
    partner_score = jnp.sum(jnp.where(partner_hit, scores, 0.0), axis=1)
    contrast_loss = jnp.mean(log_total - partner_score)

    first = row_block * group
    rows = first + jnp.arange(group, dtype=jnp.int32)
    row_scores = lax.dynamic_slice_in_dim(scores, first, group, axis=0)
    row_totals = lax.dynamic_slice_in_dim(log_total, first, group, axis=0)
    row_partner = lax.dynamic_slice_in_dim(partner, first, group, axis=0)
    row_others = rows[:, None] != batch_iota[None, :]
    row_weight = jnp.where(row_others, jnp.exp(row_scores - row_totals[:, None]), 0.0) - (
        batch_iota[None, :] == row_partner[:, None]
    ).astype(f32)
    col_scores = lax.dynamic_slice_in_dim(scores, first, group, axis=1).T
    col_weight = jnp.where(row_others, jnp.exp(col_scores - log_total[None, :]), 0.0) - (
        rows[:, None] == partner[None, :]
    ).astype(f32)
    embed_grad = (
        score_scale
        / model_width
        * jnp.dot(row_weight + col_weight, gathered.astype(f32), precision=highest)
    )
    seq_grad = (
        inv_rms[:, None] * embed_grad
        - (inv_rms**3 * jnp.sum(pooled * embed_grad, axis=1) / model_width)[:, None] * pooled
    )

    slot_dots = jnp.sum(out_f32 * seq_grad[:, None, None, :], axis=3)
    out_grad = (gates[..., None] * seq_grad[:, None, None, :]).astype(bf16)
    hidden_grad = jnp.einsum("secd,efd->secf", out_grad, down_full, preferred_element_type=f32)
    gate_side = (hidden_grad * pre_up * derivative).astype(bf16)
    up_side = (hidden_grad * activated).astype(bf16)
    route_here = jnp.einsum("secf,edf->secd", gate_side, gate_full, preferred_element_type=f32)
    route_here = (
        route_here
        + jnp.einsum("secf,edf->secd", up_side, up_full, preferred_element_type=f32)
    ).astype(bf16)
    route_here = jnp.concatenate([route_here, pack_row(slot_dots, model_width)], axis=2)
    returned = lax.all_to_all(route_here, "expert", split_axis=0, concat_axis=0, tiled=True)
    returned = returned.reshape(experts, capacity + 1, model_width)

    route_rows = returned[:, :capacity, :].reshape(slot_total, model_width)
    slot_grads = join3(returned[:, capacity, :], capacity)
    token_slot_grads = jnp.sum(jnp.where(onehot, slot_grads[:, :, None], 0.0), axis=1).T
    gate_grad = jnp.sum(jnp.where(matches, token_slot_grads[:, None, :], 0.0), axis=2)
    route_sum = jnp.einsum("st,sd->td", placer_flat, route_rows, preferred_element_type=f32)
    own_grad = lax.dynamic_index_in_dim(seq_grad, me, axis=0, keepdims=False)
    token_grad = (own_grad[None, :] + route_sum).astype(bf16)
    return (contrast_loss, token_grad, gate_grad)


def solution(mesh):
    placed = (
        P(("dp", "expert"), None),
        P(("dp", "expert"), None),
        P(("dp", "expert"), None),
        P("expert", "dp", None),
        P("expert", "dp", None),
        P("expert", "dp", None),
        P(),
    )
    return jax.shard_map(
        on_device,
        mesh=mesh,
        in_specs=placed,
        out_specs=(P(), P(("dp", "expert"), None), P(("dp", "expert"), None)),
        check_vma=False,
    )
```

```python
import jax
import jax.numpy as jnp
from jax import lax
from jax.sharding import PartitionSpec as P

score_scale = 20.0
highest = lax.Precision.HIGHEST
f32 = jnp.float32
bf16 = jnp.bfloat16


def silu_parts(pre_act):
    sigmoid_val = jax.nn.sigmoid(pre_act)
    return (pre_act * sigmoid_val, sigmoid_val * (1.0 + pre_act * (1.0 - sigmoid_val)))


def split3(x):
    hi = lax.reduce_precision(x, exponent_bits=8, mantissa_bits=7)
    rest = x - hi
    mid = lax.reduce_precision(rest, exponent_bits=8, mantissa_bits=7)
    lo = rest - mid
    return jnp.concatenate([hi, mid, lo], axis=-1).astype(bf16)


def join3(packed, n):
    hi = packed[..., :n].astype(f32)
    mid = packed[..., n : 2 * n].astype(f32)
    lo = packed[..., 2 * n : 3 * n].astype(f32)
    return hi + (mid + lo)


def pack_row(values, width):
    pieces = split3(values)
    pad = width - pieces.shape[-1]
    return jnp.pad(pieces, [(0, 0)] * (pieces.ndim - 1) + [(0, pad)])


def on_device(tokens, expert_ids, gate_values, w_gate, w_up, w_down, partner):
    tok_rows, model_width = tokens.shape
    route_count = expert_ids.shape[1]
    local_experts = w_gate.shape[0]
    group = lax.axis_size("expert")
    experts = group * local_experts
    capacity = tok_rows * route_count // experts + max(1, tok_rows * route_count // (16 * experts))
    slot_total = experts * capacity
    me = lax.axis_index("expert")
    row_block = lax.axis_index("dp")

    ff_width = w_gate.shape[2]
    stacked = jnp.stack([w_gate, w_up, w_down.reshape(w_gate.shape)])
    every = lax.all_gather(stacked, "dp", axis=2, tiled=True)
    gate_full = every[0]
    up_full = every[1]
    down_full = every[2].reshape(local_experts, ff_width, model_width)

    expert_iota = jnp.arange(experts, dtype=jnp.int32)
    matches = expert_ids[:, :, None] == expert_iota
    chosen = jnp.sum(matches.astype(jnp.int32), axis=1, dtype=jnp.int32)
    chosen_gate = jnp.sum(jnp.where(matches, gate_values[:, :, None], 0.0), axis=1)
    before = jnp.cumsum(chosen, axis=0, dtype=jnp.int32) - chosen
    slot_rank = jnp.sum(jnp.where(matches, before[:, None, :], 0), axis=2, dtype=jnp.int32)
    slot_iota = jnp.arange(capacity, dtype=jnp.int32)
    onehot = (chosen.T[:, None, :] == 1) & (before.T[:, None, :] == slot_iota[None, :, None])
    placer = jnp.pad(onehot.astype(bf16), ((0, 0), (0, 1), (0, 0)))
    slot_gate = jnp.sum(jnp.where(onehot, chosen_gate.T[:, None, :], 0.0), axis=2)
    outgoing = jnp.einsum("ect,td->ecd", placer, tokens, preferred_element_type=f32).astype(bf16)
    outgoing = outgoing.at[:, capacity, :].set(pack_row(slot_gate, model_width))
    outgoing = outgoing.reshape(group, local_experts, capacity + 1, model_width)

    arrived = lax.all_to_all(outgoing, "expert", split_axis=0, concat_axis=0, tiled=True)
    rows_in = arrived
    gates = jnp.pad(join3(arrived[:, :, capacity, :], capacity), ((0, 0), (0, 0), (0, 1)))
    pre_gate = jnp.einsum("secd,edf->secf", rows_in, gate_full, preferred_element_type=f32)
    pre_up = jnp.einsum("secd,edf->secf", rows_in, up_full, preferred_element_type=f32)
    activated, derivative = silu_parts(pre_gate)
    hidden = (activated * pre_up).astype(bf16)
    expert_out = jnp.einsum("secf,efd->secd", hidden, down_full, preferred_element_type=f32).astype(
        bf16
    )
    out_f32 = expert_out.astype(f32)
    partial = jnp.sum(gates[..., None] * out_f32, axis=(1, 2))

    token_mean = jnp.mean(tokens.astype(f32), axis=0)
    shares = lax.all_to_all(partial / tok_rows, "expert", split_axis=0, concat_axis=0, tiled=True)
    own_pooled = token_mean + jnp.sum(shares, axis=0)
    copies = jnp.broadcast_to(own_pooled[None, :], (group, model_width))
    pooled = lax.all_to_all(copies, "expert", split_axis=0, concat_axis=0, tiled=True)
    inv_rms = lax.rsqrt(jnp.mean(pooled * pooled, axis=1) + 1e-06)
    embedding = (pooled * inv_rms[:, None]).astype(bf16)
    blocks = lax.axis_size("dp")
    spread = jnp.broadcast_to(embedding[None], (blocks, group, model_width))
    gathered = lax.all_to_all(spread, "dp", split_axis=0, concat_axis=0, tiled=True)
    gathered = gathered.reshape(blocks * group, model_width)
    batch_size = gathered.shape[0]

    scores = (
        score_scale
        / model_width
        * lax.dot_general(
            gathered, gathered, (((1,), (1,)), ((), ())), preferred_element_type=f32
        )
    )
    batch_iota = jnp.arange(batch_size, dtype=jnp.int32)
    others = batch_iota[:, None] != batch_iota[None, :]
    log_total = jnp.log(jnp.sum(jnp.where(others, jnp.exp(scores), 0.0), axis=1))
    partner_hit = batch_iota[None, :] == partner[:, None]
    partner_score = jnp.sum(jnp.where(partner_hit, scores, 0.0), axis=1)
    contrast_loss = jnp.mean(log_total - partner_score)

    first = row_block * group
    rows = first + jnp.arange(group, dtype=jnp.int32)
    row_scores = lax.dynamic_slice_in_dim(scores, first, group, axis=0)
    row_totals = lax.dynamic_slice_in_dim(log_total, first, group, axis=0)
    row_partner = lax.dynamic_slice_in_dim(partner, first, group, axis=0)
    row_others = rows[:, None] != batch_iota[None, :]
    row_weight = jnp.where(row_others, jnp.exp(row_scores - row_totals[:, None]), 0.0) - (
        batch_iota[None, :] == row_partner[:, None]
    ).astype(f32)
    col_scores = lax.dynamic_slice_in_dim(scores, first, group, axis=1).T
    col_weight = jnp.where(row_others, jnp.exp(col_scores - log_total[None, :]), 0.0) - (
        rows[:, None] == partner[None, :]
    ).astype(f32)
    embed_grad = (
        score_scale
        / model_width
        * jnp.dot(row_weight + col_weight, gathered.astype(f32), precision=highest)
    )
    seq_grad = (
        inv_rms[:, None] * embed_grad
        - (inv_rms**3 * jnp.sum(pooled * embed_grad, axis=1) / model_width)[:, None] * pooled
    )

    slot_dots = jnp.sum(out_f32 * seq_grad[:, None, None, :], axis=3)
    out_grad = (gates[..., None] * seq_grad[:, None, None, :]).astype(bf16)
    hidden_grad = jnp.einsum("secd,efd->secf", out_grad, down_full, preferred_element_type=f32)
    gate_side = (hidden_grad * pre_up * derivative).astype(bf16)
    up_side = (hidden_grad * activated).astype(bf16)
    route_here = jnp.einsum("secf,edf->secd", gate_side, gate_full, preferred_element_type=f32)
    route_here = (
        route_here
        + jnp.einsum("secf,edf->secd", up_side, up_full, preferred_element_type=f32)
    ).astype(bf16)
    route_here = route_here.at[:, :, capacity, :].set(pack_row(slot_dots[:, :, :capacity], model_width))
    returned = lax.all_to_all(route_here, "expert", split_axis=0, concat_axis=0, tiled=True)
    returned = returned.reshape(experts, capacity + 1, model_width)

    slot_grads = join3(returned[:, capacity, :], capacity)
    token_slot_grads = jnp.sum(jnp.where(onehot, slot_grads[:, :, None], 0.0), axis=1).T
    gate_grad = jnp.sum(jnp.where(matches, token_slot_grads[:, None, :], 0.0), axis=2)
    route_sum = jnp.einsum("ect,ecd->td", placer, returned, preferred_element_type=f32)
    own_grad = lax.dynamic_index_in_dim(seq_grad, me, axis=0, keepdims=False)
    token_grad = (own_grad[None, :] + route_sum).astype(bf16)
    return (contrast_loss, token_grad, gate_grad)


def solution(mesh):
    placed = (
        P(("dp", "expert"), None),
        P(("dp", "expert"), None),
        P(("dp", "expert"), None),
        P("expert", "dp", None),
        P("expert", "dp", None),
        P("expert", "dp", None),
        P(),
    )
    return jax.shard_map(
        on_device,
        mesh=mesh,
        in_specs=placed,
        out_specs=(P(), P(("dp", "expert"), None), P(("dp", "expert"), None)),
        check_vma=False,
    )
```

```python
import jax
import jax.numpy as jnp
from jax import lax
from jax.sharding import PartitionSpec as P

score_scale = 20.0
highest = lax.Precision.HIGHEST
f32 = jnp.float32
bf16 = jnp.bfloat16


def silu_parts(pre_act):
    sigmoid_val = jax.nn.sigmoid(pre_act)
    return (pre_act * sigmoid_val, sigmoid_val * (1.0 + pre_act * (1.0 - sigmoid_val)))


def split3(x):
    hi = lax.reduce_precision(x, exponent_bits=8, mantissa_bits=7)
    rest = x - hi
    mid = lax.reduce_precision(rest, exponent_bits=8, mantissa_bits=7)
    lo = rest - mid
    return jnp.concatenate([hi, mid, lo], axis=-1).astype(bf16)


def join3(packed, n):
    hi = packed[..., :n].astype(f32)
    mid = packed[..., n : 2 * n].astype(f32)
    lo = packed[..., 2 * n : 3 * n].astype(f32)
    return hi + (mid + lo)


def pack_row(values, width):
    pieces = split3(values)
    pad = width - pieces.shape[-1]
    return jnp.pad(pieces, [(0, 0)] * (pieces.ndim - 1) + [(0, pad)])


def on_device(tokens, expert_ids, gate_values, w_gate, w_up, w_down, partner):
    tok_rows, model_width = tokens.shape
    route_count = expert_ids.shape[1]
    local_experts = w_gate.shape[0]
    group = lax.axis_size("expert")
    experts = group * local_experts
    capacity = tok_rows * route_count // experts + max(1, tok_rows * route_count // (16 * experts))
    slot_total = experts * capacity
    me = lax.axis_index("expert")
    row_block = lax.axis_index("dp")

    ff_width = w_gate.shape[2]
    stacked = jnp.stack([w_gate, w_up, w_down.reshape(w_gate.shape)])
    every = lax.all_gather(stacked, "dp", axis=2, tiled=True)
    gate_full = every[0]
    up_full = every[1]
    down_full = every[2].reshape(local_experts, ff_width, model_width)

    expert_iota = jnp.arange(experts, dtype=jnp.int32)
    matches = expert_ids[:, :, None] == expert_iota
    chosen = jnp.sum(matches.astype(jnp.int32), axis=1, dtype=jnp.int32)
    chosen_gate = jnp.sum(jnp.where(matches, gate_values[:, :, None], 0.0), axis=1)
    before = jnp.cumsum(chosen, axis=0, dtype=jnp.int32) - chosen
    slot_rank = jnp.sum(jnp.where(matches, before[:, None, :], 0), axis=2, dtype=jnp.int32)
    slot_iota = jnp.arange(capacity, dtype=jnp.int32)
    onehot = (chosen.T[:, None, :] == 1) & (before.T[:, None, :] == slot_iota[None, :, None])
    placer = jnp.pad(onehot.astype(bf16), ((0, 0), (0, 1), (0, 0)))
    slot_gate = jnp.sum(jnp.where(onehot, chosen_gate.T[:, None, :], 0.0), axis=2)
    placer = placer.reshape(group, local_experts, capacity + 1, tok_rows).transpose(0, 2, 1, 3)
    outgoing = jnp.einsum("jcet,td->jced", placer, tokens, preferred_element_type=f32).astype(bf16)
    gate_row = pack_row(slot_gate, model_width).reshape(group, local_experts, model_width)
    outgoing = outgoing.at[:, capacity, :, :].set(gate_row)

    arrived = lax.all_to_all(outgoing, "expert", split_axis=0, concat_axis=0, tiled=True)
    rows_in = arrived
    gates = jnp.swapaxes(join3(arrived[:, capacity, :, :], capacity), 1, 2)
    gates = jnp.pad(gates, ((0, 0), (0, 1), (0, 0)))
    pre_gate = jnp.einsum("sced,edf->scef", rows_in, gate_full, preferred_element_type=f32)
    pre_up = jnp.einsum("sced,edf->scef", rows_in, up_full, preferred_element_type=f32)
    activated, derivative = silu_parts(pre_gate)
    hidden = (activated * pre_up).astype(bf16)
    expert_out = jnp.einsum("scef,efd->sced", hidden, down_full, preferred_element_type=f32).astype(
        bf16
    )
    out_f32 = expert_out.astype(f32)
    partial = jnp.sum(gates[..., None] * out_f32, axis=(1, 2))

    token_mean = jnp.mean(tokens.astype(f32), axis=0)
    shares = lax.all_to_all(partial / tok_rows, "expert", split_axis=0, concat_axis=0, tiled=True)
    own_pooled = token_mean + jnp.sum(shares, axis=0)
    copies = jnp.broadcast_to(own_pooled[None, :], (group, model_width))
    pooled = lax.all_to_all(copies, "expert", split_axis=0, concat_axis=0, tiled=True)
    inv_rms = lax.rsqrt(jnp.mean(pooled * pooled, axis=1) + 1e-06)
    embedding = (pooled * inv_rms[:, None]).astype(bf16)
    blocks = lax.axis_size("dp")
    spread = jnp.broadcast_to(embedding[None], (blocks, group, model_width))
    gathered = lax.all_to_all(spread, "dp", split_axis=0, concat_axis=0, tiled=True)
    gathered = gathered.reshape(blocks * group, model_width)
    batch_size = gathered.shape[0]

    scores = (
        score_scale
        / model_width
        * lax.dot_general(
            gathered, gathered, (((1,), (1,)), ((), ())), preferred_element_type=f32
        )
    )
    batch_iota = jnp.arange(batch_size, dtype=jnp.int32)
    others = batch_iota[:, None] != batch_iota[None, :]
    log_total = jnp.log(jnp.sum(jnp.where(others, jnp.exp(scores), 0.0), axis=1))
    partner_hit = batch_iota[None, :] == partner[:, None]
    partner_score = jnp.sum(jnp.where(partner_hit, scores, 0.0), axis=1)
    contrast_loss = jnp.mean(log_total - partner_score)

    first = row_block * group
    rows = first + jnp.arange(group, dtype=jnp.int32)
    row_scores = lax.dynamic_slice_in_dim(scores, first, group, axis=0)
    row_totals = lax.dynamic_slice_in_dim(log_total, first, group, axis=0)
    row_partner = lax.dynamic_slice_in_dim(partner, first, group, axis=0)
    row_others = rows[:, None] != batch_iota[None, :]
    row_weight = jnp.where(row_others, jnp.exp(row_scores - row_totals[:, None]), 0.0) - (
        batch_iota[None, :] == row_partner[:, None]
    ).astype(f32)
    col_scores = lax.dynamic_slice_in_dim(scores, first, group, axis=1).T
    col_weight = jnp.where(row_others, jnp.exp(col_scores - log_total[None, :]), 0.0) - (
        rows[:, None] == partner[None, :]
    ).astype(f32)
    embed_grad = (
        score_scale
        / model_width
        * jnp.dot(row_weight + col_weight, gathered.astype(f32), precision=highest)
    )
    seq_grad = (
        inv_rms[:, None] * embed_grad
        - (inv_rms**3 * jnp.sum(pooled * embed_grad, axis=1) / model_width)[:, None] * pooled
    )

    slot_dots = jnp.sum(out_f32 * seq_grad[:, None, None, :], axis=3)
    out_grad = (gates[..., None] * seq_grad[:, None, None, :]).astype(bf16)
    hidden_grad = jnp.einsum("sced,efd->scef", out_grad, down_full, preferred_element_type=f32)
    gate_side = (hidden_grad * pre_up * derivative).astype(bf16)
    up_side = (hidden_grad * activated).astype(bf16)
    route_here = jnp.einsum("scef,edf->sced", gate_side, gate_full, preferred_element_type=f32)
    route_here = (
        route_here
        + jnp.einsum("scef,edf->sced", up_side, up_full, preferred_element_type=f32)
    ).astype(bf16)
    grad_row = pack_row(jnp.swapaxes(slot_dots[:, :capacity, :], 1, 2), model_width)
    route_here = route_here.at[:, capacity, :, :].set(grad_row)
    returned = lax.all_to_all(route_here, "expert", split_axis=0, concat_axis=0, tiled=True)

    slot_grads = join3(returned[:, capacity, :, :], capacity).reshape(experts, capacity)
    token_slot_grads = jnp.sum(jnp.where(onehot, slot_grads[:, :, None], 0.0), axis=1).T
    gate_grad = jnp.sum(jnp.where(matches, token_slot_grads[:, None, :], 0.0), axis=2)
    route_sum = jnp.einsum("jcet,jced->td", placer, returned, preferred_element_type=f32)
    own_grad = lax.dynamic_index_in_dim(seq_grad, me, axis=0, keepdims=False)
    token_grad = (own_grad[None, :] + route_sum).astype(bf16)
    return (contrast_loss, token_grad, gate_grad)


def solution(mesh):
    placed = (
        P(("dp", "expert"), None),
        P(("dp", "expert"), None),
        P(("dp", "expert"), None),
        P("expert", "dp", None),
        P("expert", "dp", None),
        P("expert", "dp", None),
        P(),
    )
    return jax.shard_map(
        on_device,
        mesh=mesh,
        in_specs=placed,
        out_specs=(P(), P(("dp", "expert"), None), P(("dp", "expert"), None)),
        check_vma=False,
    )
```

```python
import jax
import jax.numpy as jnp
from jax import lax
from jax.sharding import PartitionSpec as P

score_scale = 20.0
highest = lax.Precision.HIGHEST
f32 = jnp.float32
bf16 = jnp.bfloat16


def silu_parts(pre_act):
    sigmoid_val = jax.nn.sigmoid(pre_act)
    return (pre_act * sigmoid_val, sigmoid_val * (1.0 + pre_act * (1.0 - sigmoid_val)))


def split3(x):
    hi = lax.reduce_precision(x, exponent_bits=8, mantissa_bits=7)
    rest = x - hi
    mid = lax.reduce_precision(rest, exponent_bits=8, mantissa_bits=7)
    lo = rest - mid
    return jnp.concatenate([hi, mid, lo], axis=-1).astype(bf16)


def join3(packed, n):
    hi = packed[..., :n].astype(f32)
    mid = packed[..., n : 2 * n].astype(f32)
    lo = packed[..., 2 * n : 3 * n].astype(f32)
    return hi + (mid + lo)


def pack_row(values, width):
    pieces = split3(values)
    pad = width - pieces.shape[-1]
    return jnp.pad(pieces, [(0, 0)] * (pieces.ndim - 1) + [(0, pad)])


def butterfly_sum(x, axis, n):
    step = 1
    while step < n:
        x = x + lax.ppermute(x, axis, [(j, j ^ step) for j in range(n)])
        step *= 2
    return x


def butterfly_gather(x, axis, n):
    me = lax.axis_index(axis)
    step = 1
    while step < n:
        other = lax.ppermute(x, axis, [(j, j ^ step) for j in range(n)])
        low = (me // step) % 2 == 0
        x = jnp.where(low, jnp.concatenate([x, other]), jnp.concatenate([other, x]))
        step *= 2
    return x


def on_device(tokens, expert_ids, gate_values, w_gate, w_up, w_down, partner):
    tok_rows, model_width = tokens.shape
    route_count = expert_ids.shape[1]
    local_experts = w_gate.shape[0]
    group = lax.axis_size("expert")
    experts = group * local_experts
    capacity = tok_rows * route_count // experts + max(1, tok_rows * route_count // (16 * experts))
    slot_total = experts * capacity
    me = lax.axis_index("expert")
    row_block = lax.axis_index("dp")

    ff_width = w_gate.shape[2]
    stacked = jnp.stack([w_gate, w_up, w_down.reshape(w_gate.shape)])
    every = lax.all_gather(stacked, "dp", axis=2, tiled=True)
    gate_full = every[0]
    up_full = every[1]
    down_full = every[2].reshape(local_experts, ff_width, model_width)

    expert_iota = jnp.arange(experts, dtype=jnp.int32)
    matches = expert_ids[:, :, None] == expert_iota
    chosen = jnp.sum(matches.astype(jnp.int32), axis=1, dtype=jnp.int32)
    chosen_gate = jnp.sum(jnp.where(matches, gate_values[:, :, None], 0.0), axis=1)
    before = jnp.cumsum(chosen, axis=0, dtype=jnp.int32) - chosen
    slot_rank = jnp.sum(jnp.where(matches, before[:, None, :], 0), axis=2, dtype=jnp.int32)
    slot_iota = jnp.arange(capacity, dtype=jnp.int32)
    onehot = (chosen.T[:, None, :] == 1) & (before.T[:, None, :] == slot_iota[None, :, None])
    placer = jnp.pad(onehot.astype(bf16), ((0, 0), (0, 1), (0, 0)))
    slot_gate = jnp.sum(jnp.where(onehot, chosen_gate.T[:, None, :], 0.0), axis=2)
    placer = placer.reshape(group, local_experts, capacity + 1, tok_rows).transpose(0, 2, 1, 3)
    outgoing = jnp.einsum("jcet,td->jced", placer, tokens, preferred_element_type=f32).astype(bf16)
    gate_row = pack_row(slot_gate, model_width).reshape(group, local_experts, model_width)
    outgoing = outgoing.at[:, capacity, :, :].set(gate_row)

    arrived = lax.all_to_all(outgoing, "expert", split_axis=0, concat_axis=0, tiled=True)
    rows_in = arrived
    gates = jnp.swapaxes(join3(arrived[:, capacity, :, :], capacity), 1, 2)
    gates = jnp.pad(gates, ((0, 0), (0, 1), (0, 0)))
    pre_gate = jnp.einsum("sced,edf->scef", rows_in, gate_full, preferred_element_type=f32)
    pre_up = jnp.einsum("sced,edf->scef", rows_in, up_full, preferred_element_type=f32)
    activated, derivative = silu_parts(pre_gate)
    hidden = (activated * pre_up).astype(bf16)
    expert_out = jnp.einsum("scef,efd->sced", hidden, down_full, preferred_element_type=f32).astype(
        bf16
    )
    out_f32 = expert_out.astype(f32)
    partial = jnp.sum(gates[..., None] * out_f32, axis=(1, 2))

    token_mean = jnp.mean(tokens.astype(f32), axis=0)
    own_row = (jnp.arange(group, dtype=jnp.int32) == me)[:, None]
    share = partial / tok_rows + jnp.where(own_row, token_mean[None, :], 0.0)
    pooled = butterfly_sum(share, "expert", group)
    inv_rms = lax.rsqrt(jnp.mean(pooled * pooled, axis=1) + 1e-06)
    embedding = (pooled * inv_rms[:, None]).astype(bf16)
    blocks = lax.axis_size("dp")
    gathered = butterfly_gather(embedding, "dp", blocks)
    batch_size = gathered.shape[0]

    scores = (
        score_scale
        / model_width
        * lax.dot_general(
            gathered, gathered, (((1,), (1,)), ((), ())), preferred_element_type=f32
        )
    )
    batch_iota = jnp.arange(batch_size, dtype=jnp.int32)
    others = batch_iota[:, None] != batch_iota[None, :]
    log_total = jnp.log(jnp.sum(jnp.where(others, jnp.exp(scores), 0.0), axis=1))
    partner_hit = batch_iota[None, :] == partner[:, None]
    partner_score = jnp.sum(jnp.where(partner_hit, scores, 0.0), axis=1)
    contrast_loss = jnp.mean(log_total - partner_score)

    first = row_block * group
    rows = first + jnp.arange(group, dtype=jnp.int32)
    row_scores = lax.dynamic_slice_in_dim(scores, first, group, axis=0)
    row_totals = lax.dynamic_slice_in_dim(log_total, first, group, axis=0)
    row_partner = lax.dynamic_slice_in_dim(partner, first, group, axis=0)
    row_others = rows[:, None] != batch_iota[None, :]
    row_weight = jnp.where(row_others, jnp.exp(row_scores - row_totals[:, None]), 0.0) - (
        batch_iota[None, :] == row_partner[:, None]
    ).astype(f32)
    col_scores = lax.dynamic_slice_in_dim(scores, first, group, axis=1).T
    col_weight = jnp.where(row_others, jnp.exp(col_scores - log_total[None, :]), 0.0) - (
        rows[:, None] == partner[None, :]
    ).astype(f32)
    embed_grad = (
        score_scale
        / model_width
        * jnp.dot(row_weight + col_weight, gathered.astype(f32), precision=highest)
    )
    seq_grad = (
        inv_rms[:, None] * embed_grad
        - (inv_rms**3 * jnp.sum(pooled * embed_grad, axis=1) / model_width)[:, None] * pooled
    )

    slot_dots = jnp.sum(out_f32 * seq_grad[:, None, None, :], axis=3)
    out_grad = (gates[..., None] * seq_grad[:, None, None, :]).astype(bf16)
    hidden_grad = jnp.einsum("sced,efd->scef", out_grad, down_full, preferred_element_type=f32)
    gate_side = (hidden_grad * pre_up * derivative).astype(bf16)
    up_side = (hidden_grad * activated).astype(bf16)
    route_here = jnp.einsum("scef,edf->sced", gate_side, gate_full, preferred_element_type=f32)
    route_here = (
        route_here
        + jnp.einsum("scef,edf->sced", up_side, up_full, preferred_element_type=f32)
    ).astype(bf16)
    grad_row = pack_row(jnp.swapaxes(slot_dots[:, :capacity, :], 1, 2), model_width)
    route_here = route_here.at[:, capacity, :, :].set(grad_row)
    returned = lax.all_to_all(route_here, "expert", split_axis=0, concat_axis=0, tiled=True)

    slot_grads = join3(returned[:, capacity, :, :], capacity).reshape(experts, capacity)
    token_slot_grads = jnp.sum(jnp.where(onehot, slot_grads[:, :, None], 0.0), axis=1).T
    gate_grad = jnp.sum(jnp.where(matches, token_slot_grads[:, None, :], 0.0), axis=2)
    route_sum = jnp.einsum("jcet,jced->td", placer, returned, preferred_element_type=f32)
    own_grad = lax.dynamic_index_in_dim(seq_grad, me, axis=0, keepdims=False)
    token_grad = (own_grad[None, :] + route_sum).astype(bf16)
    return (contrast_loss, token_grad, gate_grad)


def solution(mesh):
    placed = (
        P(("dp", "expert"), None),
        P(("dp", "expert"), None),
        P(("dp", "expert"), None),
        P("expert", "dp", None),
        P("expert", "dp", None),
        P("expert", "dp", None),
        P(),
    )
    return jax.shard_map(
        on_device,
        mesh=mesh,
        in_specs=placed,
        out_specs=(P(), P(("dp", "expert"), None), P(("dp", "expert"), None)),
        check_vma=False,
    )
```

```python
import jax
import jax.numpy as jnp
from jax import lax
from jax.sharding import PartitionSpec as P

score_scale = 20.0
highest = lax.Precision.HIGHEST
f32 = jnp.float32
bf16 = jnp.bfloat16


def silu_parts(pre_act):
    sigmoid_val = jax.nn.sigmoid(pre_act)
    return (pre_act * sigmoid_val, sigmoid_val * (1.0 + pre_act * (1.0 - sigmoid_val)))


def split3(x):
    hi = lax.reduce_precision(x, exponent_bits=8, mantissa_bits=7)
    rest = x - hi
    mid = lax.reduce_precision(rest, exponent_bits=8, mantissa_bits=7)
    lo = rest - mid
    return jnp.concatenate([hi, mid, lo], axis=-1).astype(bf16)


def join3(packed, n):
    hi = packed[..., :n].astype(f32)
    mid = packed[..., n : 2 * n].astype(f32)
    lo = packed[..., 2 * n : 3 * n].astype(f32)
    return hi + (mid + lo)


def pack_row(values, width):
    pieces = split3(values)
    pad = width - pieces.shape[-1]
    return jnp.pad(pieces, [(0, 0)] * (pieces.ndim - 1) + [(0, pad)])


def on_device(tokens, expert_ids, gate_values, w_gate, w_up, w_down, partner):
    tok_rows, model_width = tokens.shape
    route_count = expert_ids.shape[1]
    local_experts = w_gate.shape[0]
    group = lax.axis_size("expert")
    experts = group * local_experts
    capacity = tok_rows * route_count // experts + max(1, tok_rows * route_count // (16 * experts))
    slot_total = experts * capacity
    me = lax.axis_index("expert")
    row_block = lax.axis_index("dp")

    ff_width = w_gate.shape[2]
    stacked = jnp.stack([w_gate, w_up, w_down.reshape(w_gate.shape)])
    every = lax.all_gather(stacked, "dp", axis=2, tiled=True)
    gate_full = every[0]
    up_full = every[1]
    down_full = every[2].reshape(local_experts, ff_width, model_width)

    expert_iota = jnp.arange(experts, dtype=jnp.int32)
    matches = expert_ids[:, :, None] == expert_iota
    chosen = jnp.sum(matches.astype(jnp.int32), axis=1, dtype=jnp.int32)
    chosen_gate = jnp.sum(jnp.where(matches, gate_values[:, :, None], 0.0), axis=1)
    before = jnp.cumsum(chosen, axis=0, dtype=jnp.int32) - chosen
    slot_rank = jnp.sum(jnp.where(matches, before[:, None, :], 0), axis=2, dtype=jnp.int32)
    slot_iota = jnp.arange(capacity, dtype=jnp.int32)
    onehot = (chosen.T[:, None, :] == 1) & (before.T[:, None, :] == slot_iota[None, :, None])
    placer = jnp.pad(onehot.astype(bf16), ((0, 0), (0, 1), (0, 0)))
    slot_gate = jnp.sum(jnp.where(onehot, chosen_gate.T[:, None, :], 0.0), axis=2)
    placer = placer.reshape(group, local_experts, capacity + 1, tok_rows).transpose(0, 2, 1, 3)
    outgoing = jnp.einsum("jcet,td->jced", placer, tokens, preferred_element_type=f32).astype(bf16)
    gate_row = pack_row(slot_gate, model_width).reshape(group, local_experts, model_width)
    outgoing = outgoing.at[:, capacity, :, :].set(gate_row)

    arrived = lax.all_to_all(outgoing, "expert", split_axis=0, concat_axis=0, tiled=True)
    rows_in = arrived
    gates = jnp.swapaxes(join3(arrived[:, capacity, :, :], capacity), 1, 2)
    gates = jnp.pad(gates, ((0, 0), (0, 1), (0, 0)))
    pre_gate = jnp.einsum("sced,edf->scef", rows_in, gate_full, preferred_element_type=f32)
    pre_up = jnp.einsum("sced,edf->scef", rows_in, up_full, preferred_element_type=f32)
    activated, derivative = silu_parts(pre_gate)
    hidden = (activated * pre_up).astype(bf16)
    expert_out = jnp.einsum("scef,efd->sced", hidden, down_full, preferred_element_type=f32).astype(
        bf16
    )
    out_f32 = expert_out.astype(f32)
    partial = jnp.sum(gates[..., None] * out_f32, axis=(1, 2))

    token_mean = jnp.mean(tokens.astype(f32), axis=0)
    shares = lax.all_to_all(partial / tok_rows, "expert", split_axis=0, concat_axis=0, tiled=True)
    own_pooled = token_mean + jnp.sum(shares, axis=0)
    blocks = lax.axis_size("dp")
    copies = jnp.broadcast_to(own_pooled[None, :], (blocks, model_width))
    column = lax.all_to_all(copies, "dp", split_axis=0, concat_axis=0, tiled=True)
    column_inv = lax.rsqrt(jnp.mean(column * column, axis=1) + 1e-06)
    column_embed = (column * column_inv[:, None]).astype(bf16)
    own_pieces = split3(own_pooled[None, :]).reshape(3, model_width)
    payload = jnp.concatenate([column_embed, own_pieces], axis=0)
    payload = jnp.broadcast_to(payload[None], (group,) + payload.shape)
    received = lax.all_to_all(payload, "expert", split_axis=0, concat_axis=0, tiled=True)
    gathered = jnp.swapaxes(received[:, :blocks, :], 0, 1).reshape(blocks * group, model_width)
    pieces = received[:, blocks:, :].astype(f32)
    pooled = pieces[:, 0, :] + (pieces[:, 1, :] + pieces[:, 2, :])
    inv_rms = lax.rsqrt(jnp.mean(pooled * pooled, axis=1) + 1e-06)
    batch_size = gathered.shape[0]

    scores = (
        score_scale
        / model_width
        * lax.dot_general(
            gathered, gathered, (((1,), (1,)), ((), ())), preferred_element_type=f32
        )
    )
    batch_iota = jnp.arange(batch_size, dtype=jnp.int32)
    others = batch_iota[:, None] != batch_iota[None, :]
    log_total = jnp.log(jnp.sum(jnp.where(others, jnp.exp(scores), 0.0), axis=1))
    partner_hit = batch_iota[None, :] == partner[:, None]
    partner_score = jnp.sum(jnp.where(partner_hit, scores, 0.0), axis=1)
    contrast_loss = jnp.mean(log_total - partner_score)

    first = row_block * group
    rows = first + jnp.arange(group, dtype=jnp.int32)
    row_scores = lax.dynamic_slice_in_dim(scores, first, group, axis=0)
    row_totals = lax.dynamic_slice_in_dim(log_total, first, group, axis=0)
    row_partner = lax.dynamic_slice_in_dim(partner, first, group, axis=0)
    row_others = rows[:, None] != batch_iota[None, :]
    row_weight = jnp.where(row_others, jnp.exp(row_scores - row_totals[:, None]), 0.0) - (
        batch_iota[None, :] == row_partner[:, None]
    ).astype(f32)
    col_scores = lax.dynamic_slice_in_dim(scores, first, group, axis=1).T
    col_weight = jnp.where(row_others, jnp.exp(col_scores - log_total[None, :]), 0.0) - (
        rows[:, None] == partner[None, :]
    ).astype(f32)
    embed_grad = (
        score_scale
        / model_width
        * jnp.dot(row_weight + col_weight, gathered.astype(f32), precision=highest)
    )
    seq_grad = (
        inv_rms[:, None] * embed_grad
        - (inv_rms**3 * jnp.sum(pooled * embed_grad, axis=1) / model_width)[:, None] * pooled
    )

    slot_dots = jnp.sum(out_f32 * seq_grad[:, None, None, :], axis=3)
    out_grad = (gates[..., None] * seq_grad[:, None, None, :]).astype(bf16)
    hidden_grad = jnp.einsum("sced,efd->scef", out_grad, down_full, preferred_element_type=f32)
    gate_side = (hidden_grad * pre_up * derivative).astype(bf16)
    up_side = (hidden_grad * activated).astype(bf16)
    route_here = jnp.einsum("scef,edf->sced", gate_side, gate_full, preferred_element_type=f32)
    route_here = (
        route_here
        + jnp.einsum("scef,edf->sced", up_side, up_full, preferred_element_type=f32)
    ).astype(bf16)
    grad_row = pack_row(jnp.swapaxes(slot_dots[:, :capacity, :], 1, 2), model_width)
    route_here = route_here.at[:, capacity, :, :].set(grad_row)
    returned = lax.all_to_all(route_here, "expert", split_axis=0, concat_axis=0, tiled=True)

    slot_grads = join3(returned[:, capacity, :, :], capacity).reshape(experts, capacity)
    token_slot_grads = jnp.sum(jnp.where(onehot, slot_grads[:, :, None], 0.0), axis=1).T
    gate_grad = jnp.sum(jnp.where(matches, token_slot_grads[:, None, :], 0.0), axis=2)
    route_sum = jnp.einsum("jcet,jced->td", placer, returned, preferred_element_type=f32)
    own_grad = lax.dynamic_index_in_dim(seq_grad, me, axis=0, keepdims=False)
    token_grad = (own_grad[None, :] + route_sum).astype(bf16)
    return (contrast_loss, token_grad, gate_grad)


def solution(mesh):
    placed = (
        P(("dp", "expert"), None),
        P(("dp", "expert"), None),
        P(("dp", "expert"), None),
        P("expert", "dp", None),
        P("expert", "dp", None),
        P("expert", "dp", None),
        P(),
    )
    return jax.shard_map(
        on_device,
        mesh=mesh,
        in_specs=placed,
        out_specs=(P(), P(("dp", "expert"), None), P(("dp", "expert"), None)),
        check_vma=False,
    )
```

```python
import jax
import jax.numpy as jnp
from jax import lax
from jax.sharding import PartitionSpec as P

score_scale = 20.0
highest = lax.Precision.HIGHEST
f32 = jnp.float32
bf16 = jnp.bfloat16


def silu_parts(pre_act):
    sigmoid_val = jax.nn.sigmoid(pre_act)
    return (pre_act * sigmoid_val, sigmoid_val * (1.0 + pre_act * (1.0 - sigmoid_val)))


def split3(x):
    hi = lax.reduce_precision(x, exponent_bits=8, mantissa_bits=7)
    rest = x - hi
    mid = lax.reduce_precision(rest, exponent_bits=8, mantissa_bits=7)
    lo = rest - mid
    return jnp.concatenate([hi, mid, lo], axis=-1).astype(bf16)


def join3(packed, n):
    hi = packed[..., :n].astype(f32)
    mid = packed[..., n : 2 * n].astype(f32)
    lo = packed[..., 2 * n : 3 * n].astype(f32)
    return hi + (mid + lo)


def pack_row(values, width):
    pieces = split3(values)
    pad = width - pieces.shape[-1]
    return jnp.pad(pieces, [(0, 0)] * (pieces.ndim - 1) + [(0, pad)])


def on_device(tokens, expert_ids, gate_values, w_gate, w_up, w_down, partner):
    tok_rows, model_width = tokens.shape
    route_count = expert_ids.shape[1]
    local_experts = w_gate.shape[0]
    group = lax.axis_size("expert")
    experts = group * local_experts
    capacity = tok_rows * route_count // experts + max(1, tok_rows * route_count // (16 * experts))
    slot_total = experts * capacity
    me = lax.axis_index("expert")
    row_block = lax.axis_index("dp")

    ff_width = w_gate.shape[2]
    stacked = jnp.concatenate([w_gate, w_up, w_down.reshape(w_gate.shape)], axis=2)
    every = lax.all_gather(stacked, "dp", axis=1, tiled=True)
    gate_up_full = every[:, :, : 2 * ff_width]
    down_full = every[:, :, 2 * ff_width :].reshape(local_experts, ff_width, model_width)

    expert_iota = jnp.arange(experts, dtype=jnp.int32)
    matches = expert_ids[:, :, None] == expert_iota
    chosen = jnp.sum(matches.astype(jnp.int32), axis=1, dtype=jnp.int32)
    chosen_gate = jnp.sum(jnp.where(matches, gate_values[:, :, None], 0.0), axis=1)
    before = jnp.cumsum(chosen, axis=0, dtype=jnp.int32) - chosen
    slot_rank = jnp.sum(jnp.where(matches, before[:, None, :], 0), axis=2, dtype=jnp.int32)
    slot_iota = jnp.arange(capacity, dtype=jnp.int32)
    onehot = (chosen.T[:, None, :] == 1) & (before.T[:, None, :] == slot_iota[None, :, None])
    placer = jnp.pad(onehot.astype(bf16), ((0, 0), (0, 1), (0, 0)))
    slot_gate = jnp.sum(jnp.where(onehot, chosen_gate.T[:, None, :], 0.0), axis=2)
    placer = placer.reshape(group, local_experts, capacity + 1, tok_rows).transpose(0, 2, 1, 3)
    outgoing = jnp.einsum("jcet,td->jced", placer, tokens, preferred_element_type=f32).astype(bf16)
    gate_row = pack_row(slot_gate, model_width).reshape(group, local_experts, model_width)
    outgoing = outgoing.at[:, capacity, :, :].set(gate_row)

    arrived = lax.all_to_all(outgoing, "expert", split_axis=0, concat_axis=0, tiled=True)
    rows_in = arrived
    gates = jnp.swapaxes(join3(arrived[:, capacity, :, :], capacity), 1, 2)
    gates = jnp.pad(gates, ((0, 0), (0, 1), (0, 0)))
    pre_both = jnp.einsum("sced,edf->scef", rows_in, gate_up_full, preferred_element_type=f32)
    pre_gate = pre_both[..., :ff_width]
    pre_up = pre_both[..., ff_width:]
    activated, derivative = silu_parts(pre_gate)
    hidden = (activated * pre_up).astype(bf16)
    expert_out = jnp.einsum("scef,efd->sced", hidden, down_full, preferred_element_type=f32).astype(
        bf16
    )
    out_f32 = expert_out.astype(f32)
    partial = jnp.sum(gates[..., None] * out_f32, axis=(1, 2))

    token_mean = jnp.mean(tokens.astype(f32), axis=0)
    shares = lax.all_to_all(partial / tok_rows, "expert", split_axis=0, concat_axis=0, tiled=True)
    own_pooled = token_mean + jnp.sum(shares, axis=0)
    copies = jnp.broadcast_to(own_pooled[None, :], (group, model_width))
    pooled = lax.all_to_all(copies, "expert", split_axis=0, concat_axis=0, tiled=True)
    inv_rms = lax.rsqrt(jnp.mean(pooled * pooled, axis=1) + 1e-06)
    embedding = (pooled * inv_rms[:, None]).astype(bf16)
    blocks = lax.axis_size("dp")
    spread = jnp.broadcast_to(embedding[None], (blocks, group, model_width))
    gathered = lax.all_to_all(spread, "dp", split_axis=0, concat_axis=0, tiled=True)
    gathered = gathered.reshape(blocks * group, model_width)
    batch_size = gathered.shape[0]

    scores = (
        score_scale
        / model_width
        * lax.dot_general(
            gathered, gathered, (((1,), (1,)), ((), ())), preferred_element_type=f32
        )
    )
    batch_iota = jnp.arange(batch_size, dtype=jnp.int32)
    others = batch_iota[:, None] != batch_iota[None, :]
    log_total = jnp.log(jnp.sum(jnp.where(others, jnp.exp(scores), 0.0), axis=1))
    partner_hit = batch_iota[None, :] == partner[:, None]
    partner_score = jnp.sum(jnp.where(partner_hit, scores, 0.0), axis=1)
    contrast_loss = jnp.mean(log_total - partner_score)

    first = row_block * group
    rows = first + jnp.arange(group, dtype=jnp.int32)
    row_scores = lax.dynamic_slice_in_dim(scores, first, group, axis=0)
    row_totals = lax.dynamic_slice_in_dim(log_total, first, group, axis=0)
    row_partner = lax.dynamic_slice_in_dim(partner, first, group, axis=0)
    row_others = rows[:, None] != batch_iota[None, :]
    row_weight = jnp.where(row_others, jnp.exp(row_scores - row_totals[:, None]), 0.0) - (
        batch_iota[None, :] == row_partner[:, None]
    ).astype(f32)
    col_scores = lax.dynamic_slice_in_dim(scores, first, group, axis=1).T
    col_weight = jnp.where(row_others, jnp.exp(col_scores - log_total[None, :]), 0.0) - (
        rows[:, None] == partner[None, :]
    ).astype(f32)
    embed_grad = (
        score_scale
        / model_width
        * jnp.dot(row_weight + col_weight, gathered.astype(f32), precision=highest)
    )
    seq_grad = (
        inv_rms[:, None] * embed_grad
        - (inv_rms**3 * jnp.sum(pooled * embed_grad, axis=1) / model_width)[:, None] * pooled
    )

    slot_dots = jnp.sum(out_f32 * seq_grad[:, None, None, :], axis=3)
    out_grad = (gates[..., None] * seq_grad[:, None, None, :]).astype(bf16)
    hidden_grad = jnp.einsum("sced,efd->scef", out_grad, down_full, preferred_element_type=f32)
    gate_side = (hidden_grad * pre_up * derivative).astype(bf16)
    up_side = (hidden_grad * activated).astype(bf16)
    both_sides = jnp.concatenate([gate_side, up_side], axis=3)
    route_here = jnp.einsum(
        "scef,edf->sced", both_sides, gate_up_full, preferred_element_type=f32
    ).astype(bf16)
    grad_row = pack_row(jnp.swapaxes(slot_dots[:, :capacity, :], 1, 2), model_width)
    route_here = route_here.at[:, capacity, :, :].set(grad_row)
    returned = lax.all_to_all(route_here, "expert", split_axis=0, concat_axis=0, tiled=True)

    slot_grads = join3(returned[:, capacity, :, :], capacity).reshape(experts, capacity)
    token_slot_grads = jnp.sum(jnp.where(onehot, slot_grads[:, :, None], 0.0), axis=1).T
    gate_grad = jnp.sum(jnp.where(matches, token_slot_grads[:, None, :], 0.0), axis=2)
    route_sum = jnp.einsum("jcet,jced->td", placer, returned, preferred_element_type=f32)
    own_grad = lax.dynamic_index_in_dim(seq_grad, me, axis=0, keepdims=False)
    token_grad = (own_grad[None, :] + route_sum).astype(bf16)
    return (contrast_loss, token_grad, gate_grad)


def solution(mesh):
    placed = (
        P(("dp", "expert"), None),
        P(("dp", "expert"), None),
        P(("dp", "expert"), None),
        P("expert", "dp", None),
        P("expert", "dp", None),
        P("expert", "dp", None),
        P(),
    )
    return jax.shard_map(
        on_device,
        mesh=mesh,
        in_specs=placed,
        out_specs=(P(), P(("dp", "expert"), None), P(("dp", "expert"), None)),
        check_vma=False,
    )
```

```python
import jax
import jax.numpy as jnp
from jax import lax
from jax.sharding import PartitionSpec as P

score_scale = 20.0
highest = lax.Precision.HIGHEST
f32 = jnp.float32
bf16 = jnp.bfloat16


def silu_parts(pre_act):
    sigmoid_val = jax.nn.sigmoid(pre_act)
    return (pre_act * sigmoid_val, sigmoid_val * (1.0 + pre_act * (1.0 - sigmoid_val)))


def split3(x):
    hi = lax.reduce_precision(x, exponent_bits=8, mantissa_bits=7)
    rest = x - hi
    mid = lax.reduce_precision(rest, exponent_bits=8, mantissa_bits=7)
    lo = rest - mid
    return jnp.concatenate([hi, mid, lo], axis=-1).astype(bf16)


def join3(packed, n):
    hi = packed[..., :n].astype(f32)
    mid = packed[..., n : 2 * n].astype(f32)
    lo = packed[..., 2 * n : 3 * n].astype(f32)
    return hi + (mid + lo)


def pack_row(values, width):
    pieces = split3(values)
    pad = width - pieces.shape[-1]
    return jnp.pad(pieces, [(0, 0)] * (pieces.ndim - 1) + [(0, pad)])


def gather_all(x, axis, n):
    me = lax.axis_index(axis)
    blocks = [x]
    for k in range(1, n):
        blocks.append(lax.ppermute(x, axis, [(p, (p - k) % n) for p in range(n)]))
    held = jnp.stack(blocks)
    doubled = jnp.concatenate([held, held])
    return lax.dynamic_slice_in_dim(doubled, n - me, n, axis=0)


def on_device(tokens, expert_ids, gate_values, w_gate, w_up, w_down, partner):
    tok_rows, model_width = tokens.shape
    route_count = expert_ids.shape[1]
    local_experts = w_gate.shape[0]
    group = lax.axis_size("expert")
    experts = group * local_experts
    capacity = tok_rows * route_count // experts + max(1, tok_rows * route_count // (16 * experts))
    slot_total = experts * capacity
    me = lax.axis_index("expert")
    row_block = lax.axis_index("dp")

    ff_width = w_gate.shape[2]
    stacked = jnp.stack([w_gate, w_up, w_down.reshape(w_gate.shape)])
    every = lax.all_gather(stacked, "dp", axis=2, tiled=True)
    gate_full = every[0]
    up_full = every[1]
    down_full = every[2].reshape(local_experts, ff_width, model_width)

    expert_iota = jnp.arange(experts, dtype=jnp.int32)
    matches = expert_ids[:, :, None] == expert_iota
    chosen = jnp.sum(matches.astype(jnp.int32), axis=1, dtype=jnp.int32)
    chosen_gate = jnp.sum(jnp.where(matches, gate_values[:, :, None], 0.0), axis=1)
    before = jnp.cumsum(chosen, axis=0, dtype=jnp.int32) - chosen
    slot_rank = jnp.sum(jnp.where(matches, before[:, None, :], 0), axis=2, dtype=jnp.int32)
    slot_iota = jnp.arange(capacity, dtype=jnp.int32)
    onehot = (chosen.T[:, None, :] == 1) & (before.T[:, None, :] == slot_iota[None, :, None])
    placer = jnp.pad(onehot.astype(bf16), ((0, 0), (0, 1), (0, 0)))
    slot_gate = jnp.sum(jnp.where(onehot, chosen_gate.T[:, None, :], 0.0), axis=2)
    placer = placer.reshape(group, local_experts, capacity + 1, tok_rows).transpose(0, 2, 1, 3)
    outgoing = jnp.einsum("jcet,td->jced", placer, tokens, preferred_element_type=f32).astype(bf16)
    gate_row = pack_row(slot_gate, model_width).reshape(group, local_experts, model_width)
    outgoing = outgoing.at[:, capacity, :, :].set(gate_row)

    arrived = lax.all_to_all(outgoing, "expert", split_axis=0, concat_axis=0, tiled=True)
    rows_in = arrived
    gates = jnp.swapaxes(join3(arrived[:, capacity, :, :], capacity), 1, 2)
    gates = jnp.pad(gates, ((0, 0), (0, 1), (0, 0)))
    pre_gate = jnp.einsum("sced,edf->scef", rows_in, gate_full, preferred_element_type=f32)
    pre_up = jnp.einsum("sced,edf->scef", rows_in, up_full, preferred_element_type=f32)
    activated, derivative = silu_parts(pre_gate)
    hidden = (activated * pre_up).astype(bf16)
    expert_out = jnp.einsum("scef,efd->sced", hidden, down_full, preferred_element_type=f32).astype(
        bf16
    )
    out_f32 = expert_out.astype(f32)
    partial = jnp.sum(gates[..., None] * out_f32, axis=(1, 2))

    token_mean = jnp.mean(tokens.astype(f32), axis=0)
    shares = lax.all_to_all(partial / tok_rows, "expert", split_axis=0, concat_axis=0, tiled=True)
    own_pooled = token_mean + jnp.sum(shares, axis=0)
    copies = jnp.broadcast_to(own_pooled[None, :], (group, model_width))
    pooled = lax.all_to_all(copies, "expert", split_axis=0, concat_axis=0, tiled=True)
    inv_rms = lax.rsqrt(jnp.mean(pooled * pooled, axis=1) + 1e-06)
    embedding = (pooled * inv_rms[:, None]).astype(bf16)
    blocks = lax.axis_size("dp")
    gathered = gather_all(embedding, "dp", blocks).reshape(blocks * group, model_width)
    batch_size = gathered.shape[0]

    scores = (
        score_scale
        / model_width
        * lax.dot_general(
            gathered, gathered, (((1,), (1,)), ((), ())), preferred_element_type=f32
        )
    )
    batch_iota = jnp.arange(batch_size, dtype=jnp.int32)
    others = batch_iota[:, None] != batch_iota[None, :]
    log_total = jnp.log(jnp.sum(jnp.where(others, jnp.exp(scores), 0.0), axis=1))
    partner_hit = batch_iota[None, :] == partner[:, None]
    partner_score = jnp.sum(jnp.where(partner_hit, scores, 0.0), axis=1)
    contrast_loss = jnp.mean(log_total - partner_score)

    first = row_block * group
    rows = first + jnp.arange(group, dtype=jnp.int32)
    row_scores = lax.dynamic_slice_in_dim(scores, first, group, axis=0)
    row_totals = lax.dynamic_slice_in_dim(log_total, first, group, axis=0)
    row_partner = lax.dynamic_slice_in_dim(partner, first, group, axis=0)
    row_others = rows[:, None] != batch_iota[None, :]
    row_weight = jnp.where(row_others, jnp.exp(row_scores - row_totals[:, None]), 0.0) - (
        batch_iota[None, :] == row_partner[:, None]
    ).astype(f32)
    col_scores = lax.dynamic_slice_in_dim(scores, first, group, axis=1).T
    col_weight = jnp.where(row_others, jnp.exp(col_scores - log_total[None, :]), 0.0) - (
        rows[:, None] == partner[None, :]
    ).astype(f32)
    embed_grad = (
        score_scale
        / model_width
        * jnp.dot(row_weight + col_weight, gathered.astype(f32), precision=highest)
    )
    seq_grad = (
        inv_rms[:, None] * embed_grad
        - (inv_rms**3 * jnp.sum(pooled * embed_grad, axis=1) / model_width)[:, None] * pooled
    )

    slot_dots = jnp.sum(out_f32 * seq_grad[:, None, None, :], axis=3)
    out_grad = (gates[..., None] * seq_grad[:, None, None, :]).astype(bf16)
    hidden_grad = jnp.einsum("sced,efd->scef", out_grad, down_full, preferred_element_type=f32)
    gate_side = (hidden_grad * pre_up * derivative).astype(bf16)
    up_side = (hidden_grad * activated).astype(bf16)
    route_here = jnp.einsum("scef,edf->sced", gate_side, gate_full, preferred_element_type=f32)
    route_here = (
        route_here
        + jnp.einsum("scef,edf->sced", up_side, up_full, preferred_element_type=f32)
    ).astype(bf16)
    grad_row = pack_row(jnp.swapaxes(slot_dots[:, :capacity, :], 1, 2), model_width)
    route_here = route_here.at[:, capacity, :, :].set(grad_row)
    returned = lax.all_to_all(route_here, "expert", split_axis=0, concat_axis=0, tiled=True)

    slot_grads = join3(returned[:, capacity, :, :], capacity).reshape(experts, capacity)
    token_slot_grads = jnp.sum(jnp.where(onehot, slot_grads[:, :, None], 0.0), axis=1).T
    gate_grad = jnp.sum(jnp.where(matches, token_slot_grads[:, None, :], 0.0), axis=2)
    route_sum = jnp.einsum("jcet,jced->td", placer, returned, preferred_element_type=f32)
    own_grad = lax.dynamic_index_in_dim(seq_grad, me, axis=0, keepdims=False)
    token_grad = (own_grad[None, :] + route_sum).astype(bf16)
    return (contrast_loss, token_grad, gate_grad)


def solution(mesh):
    placed = (
        P(("dp", "expert"), None),
        P(("dp", "expert"), None),
        P(("dp", "expert"), None),
        P("expert", "dp", None),
        P("expert", "dp", None),
        P("expert", "dp", None),
        P(),
    )
    return jax.shard_map(
        on_device,
        mesh=mesh,
        in_specs=placed,
        out_specs=(P(), P(("dp", "expert"), None), P(("dp", "expert"), None)),
        check_vma=False,
    )
```

```python
import jax
import jax.numpy as jnp
from jax import lax
from jax.sharding import PartitionSpec as P

score_scale = 20.0
highest = lax.Precision.HIGHEST
f32 = jnp.float32
bf16 = jnp.bfloat16


def silu_parts(pre_act):
    sigmoid_val = jax.nn.sigmoid(pre_act)
    return (pre_act * sigmoid_val, sigmoid_val * (1.0 + pre_act * (1.0 - sigmoid_val)))


def split3(x):
    hi = lax.reduce_precision(x, exponent_bits=8, mantissa_bits=7)
    rest = x - hi
    mid = lax.reduce_precision(rest, exponent_bits=8, mantissa_bits=7)
    lo = rest - mid
    return jnp.concatenate([hi, mid, lo], axis=-1).astype(bf16)


def join3(packed, n):
    hi = packed[..., :n].astype(f32)
    mid = packed[..., n : 2 * n].astype(f32)
    lo = packed[..., 2 * n : 3 * n].astype(f32)
    return hi + (mid + lo)


def pack_row(values, width):
    pieces = split3(values)
    pad = width - pieces.shape[-1]
    return jnp.pad(pieces, [(0, 0)] * (pieces.ndim - 1) + [(0, pad)])


def on_device(tokens, expert_ids, gate_values, w_gate, w_up, w_down, partner):
    tok_rows, model_width = tokens.shape
    route_count = expert_ids.shape[1]
    local_experts = w_gate.shape[0]
    group = lax.axis_size("expert")
    experts = group * local_experts
    capacity = tok_rows * route_count // experts + max(1, tok_rows * route_count // (16 * experts))
    slot_total = experts * capacity
    me = lax.axis_index("expert")
    row_block = lax.axis_index("dp")

    ff_width = w_gate.shape[2]
    stacked = jnp.stack([w_gate, w_up, w_down.reshape(w_gate.shape)])
    every = lax.all_gather(stacked, "dp", axis=2, tiled=True)
    gate_full = every[0]
    up_full = every[1]
    down_full = every[2].reshape(local_experts, ff_width, model_width)

    expert_iota = jnp.arange(experts, dtype=jnp.int32)
    matches = expert_ids[:, :, None] == expert_iota
    chosen = jnp.sum(matches.astype(jnp.int32), axis=1, dtype=jnp.int32)
    chosen_gate = jnp.sum(jnp.where(matches, gate_values[:, :, None], 0.0), axis=1)
    before = jnp.cumsum(chosen, axis=0, dtype=jnp.int32) - chosen
    slot_rank = jnp.sum(jnp.where(matches, before[:, None, :], 0), axis=2, dtype=jnp.int32)
    slot_iota = jnp.arange(capacity, dtype=jnp.int32)
    onehot = (chosen.T[:, None, :] == 1) & (before.T[:, None, :] == slot_iota[None, :, None])
    placer = jnp.pad(onehot.astype(bf16), ((0, 0), (0, 1), (0, 0)))
    slot_gate = jnp.sum(jnp.where(onehot, chosen_gate.T[:, None, :], 0.0), axis=2)
    placer = placer.reshape(group, local_experts, capacity + 1, tok_rows).transpose(0, 2, 1, 3)
    outgoing = jnp.einsum("jcet,td->jced", placer, tokens, preferred_element_type=f32).astype(bf16)
    gate_row = pack_row(slot_gate, model_width).reshape(group, local_experts, model_width)
    outgoing = outgoing.at[:, capacity, :, :].set(gate_row)

    arrived = lax.all_to_all(outgoing, "expert", split_axis=0, concat_axis=0, tiled=True)
    rows_in = arrived
    gates = jnp.swapaxes(join3(arrived[:, capacity, :, :], capacity), 1, 2)
    gates = jnp.pad(gates, ((0, 0), (0, 1), (0, 0)))
    pre_gate = jnp.einsum("sced,edf->scef", rows_in, gate_full, preferred_element_type=f32)
    pre_up = jnp.einsum("sced,edf->scef", rows_in, up_full, preferred_element_type=f32)
    activated, derivative = silu_parts(pre_gate)
    hidden = (activated * pre_up).astype(bf16)
    expert_out = jnp.einsum("scef,efd->sced", hidden, down_full, preferred_element_type=f32).astype(
        bf16
    )
    out_f32 = expert_out.astype(f32)
    partial = jnp.sum(gates[..., None] * out_f32, axis=(1, 2))

    token_mean = jnp.mean(tokens.astype(f32), axis=0)
    shares = lax.all_to_all(partial / tok_rows, "expert", split_axis=0, concat_axis=0, tiled=True)
    own_pooled = token_mean + jnp.sum(shares, axis=0)
    copies = jnp.broadcast_to(own_pooled[None, :], (group, model_width))
    pooled = lax.all_to_all(copies, "expert", split_axis=0, concat_axis=0, tiled=True)
    inv_rms = lax.rsqrt(jnp.mean(pooled * pooled, axis=1) + 1e-06)
    embedding = (pooled * inv_rms[:, None]).astype(bf16)
    blocks = lax.axis_size("dp")
    spread = jnp.broadcast_to(embedding[None], (blocks, group, model_width))
    gathered = lax.all_to_all(spread, "dp", split_axis=0, concat_axis=0, tiled=True)
    gathered = gathered.reshape(blocks * group, model_width)
    batch_size = gathered.shape[0]

    scores = (
        score_scale
        / model_width
        * lax.dot_general(
            gathered, gathered, (((1,), (1,)), ((), ())), preferred_element_type=f32
        )
    )
    batch_iota = jnp.arange(batch_size, dtype=jnp.int32)
    others = batch_iota[:, None] != batch_iota[None, :]
    log_total = jnp.log(jnp.sum(jnp.where(others, jnp.exp(scores), 0.0), axis=1))
    partner_hit = batch_iota[None, :] == partner[:, None]
    partner_score = jnp.sum(jnp.where(partner_hit, scores, 0.0), axis=1)
    contrast_loss = jnp.mean(log_total - partner_score)

    first = row_block * group
    rows = first + jnp.arange(group, dtype=jnp.int32)
    row_scores = lax.dynamic_slice_in_dim(scores, first, group, axis=0)
    row_totals = lax.dynamic_slice_in_dim(log_total, first, group, axis=0)
    row_partner = lax.dynamic_slice_in_dim(partner, first, group, axis=0)
    row_others = rows[:, None] != batch_iota[None, :]
    row_weight = jnp.where(row_others, jnp.exp(row_scores - row_totals[:, None]), 0.0) - (
        batch_iota[None, :] == row_partner[:, None]
    ).astype(f32)
    col_weight = jnp.where(row_others, jnp.exp(row_scores - log_total[None, :]), 0.0) - (
        rows[:, None] == partner[None, :]
    ).astype(f32)
    embed_grad = (
        score_scale
        / model_width
        * jnp.dot(row_weight + col_weight, gathered.astype(f32), precision=highest)
    )
    seq_grad = (
        inv_rms[:, None] * embed_grad
        - (inv_rms**3 * jnp.sum(pooled * embed_grad, axis=1) / model_width)[:, None] * pooled
    )

    slot_dots = jnp.sum(out_f32 * seq_grad[:, None, None, :], axis=3)
    out_grad = (gates[..., None] * seq_grad[:, None, None, :]).astype(bf16)
    hidden_grad = jnp.einsum("sced,efd->scef", out_grad, down_full, preferred_element_type=f32)
    gate_side = (hidden_grad * pre_up * derivative).astype(bf16)
    up_side = (hidden_grad * activated).astype(bf16)
    route_here = jnp.einsum("scef,edf->sced", gate_side, gate_full, preferred_element_type=f32)
    route_here = (
        route_here
        + jnp.einsum("scef,edf->sced", up_side, up_full, preferred_element_type=f32)
    ).astype(bf16)
    grad_row = pack_row(jnp.swapaxes(slot_dots[:, :capacity, :], 1, 2), model_width)
    route_here = route_here.at[:, capacity, :, :].set(grad_row)
    returned = lax.all_to_all(route_here, "expert", split_axis=0, concat_axis=0, tiled=True)

    slot_grads = join3(returned[:, capacity, :, :], capacity).reshape(experts, capacity)
    token_slot_grads = jnp.sum(jnp.where(onehot, slot_grads[:, :, None], 0.0), axis=1).T
    gate_grad = jnp.sum(jnp.where(matches, token_slot_grads[:, None, :], 0.0), axis=2)
    route_sum = jnp.einsum("jcet,jced->td", placer, returned, preferred_element_type=f32)
    own_grad = lax.dynamic_index_in_dim(seq_grad, me, axis=0, keepdims=False)
    token_grad = (own_grad[None, :] + route_sum).astype(bf16)
    return (contrast_loss, token_grad, gate_grad)


def solution(mesh):
    placed = (
        P(("dp", "expert"), None),
        P(("dp", "expert"), None),
        P(("dp", "expert"), None),
        P("expert", "dp", None),
        P("expert", "dp", None),
        P("expert", "dp", None),
        P(),
    )
    return jax.shard_map(
        on_device,
        mesh=mesh,
        in_specs=placed,
        out_specs=(P(), P(("dp", "expert"), None), P(("dp", "expert"), None)),
        check_vma=False,
    )
```

```python
import jax
import jax.numpy as jnp
from jax import lax
from jax.sharding import PartitionSpec as P

score_scale = 20.0
highest = lax.Precision.HIGHEST
f32 = jnp.float32
bf16 = jnp.bfloat16


def silu_parts(pre_act):
    sigmoid_val = jax.nn.sigmoid(pre_act)
    return (pre_act * sigmoid_val, sigmoid_val * (1.0 + pre_act * (1.0 - sigmoid_val)))


def split3(x):
    hi = lax.reduce_precision(x, exponent_bits=8, mantissa_bits=7)
    rest = x - hi
    mid = lax.reduce_precision(rest, exponent_bits=8, mantissa_bits=7)
    lo = rest - mid
    return jnp.concatenate([hi, mid, lo], axis=-1).astype(bf16)


def join3(packed, n):
    hi = packed[..., :n].astype(f32)
    mid = packed[..., n : 2 * n].astype(f32)
    lo = packed[..., 2 * n : 3 * n].astype(f32)
    return hi + (mid + lo)


def pack_row(values, width):
    pieces = split3(values)
    pad = width - pieces.shape[-1]
    return jnp.pad(pieces, [(0, 0)] * (pieces.ndim - 1) + [(0, pad)])


def on_device(tokens, expert_ids, gate_values, w_gate, w_up, w_down, partner):
    tok_rows, model_width = tokens.shape
    route_count = expert_ids.shape[1]
    local_experts = w_gate.shape[0]
    group = lax.axis_size("expert")
    experts = group * local_experts
    capacity = tok_rows * route_count // experts + max(1, tok_rows * route_count // (16 * experts))
    slot_total = experts * capacity
    me = lax.axis_index("expert")
    row_block = lax.axis_index("dp")

    ff_width = w_gate.shape[2]
    stacked = jnp.stack([w_gate, w_up, w_down.reshape(w_gate.shape)])
    every = lax.all_gather(stacked, "dp", axis=2, tiled=True)
    gate_full = every[0]
    up_full = every[1]
    down_full = every[2].reshape(local_experts, ff_width, model_width)

    expert_iota = jnp.arange(experts, dtype=jnp.int32)
    matches = expert_ids[:, :, None] == expert_iota
    chosen = jnp.sum(matches.astype(jnp.int32), axis=1, dtype=jnp.int32)
    chosen_gate = jnp.sum(jnp.where(matches, gate_values[:, :, None], 0.0), axis=1)
    before = jnp.cumsum(chosen, axis=0, dtype=jnp.int32) - chosen
    slot_rank = jnp.sum(jnp.where(matches, before[:, None, :], 0), axis=2, dtype=jnp.int32)
    slot_iota = jnp.arange(capacity, dtype=jnp.int32)
    onehot = (chosen.T[:, None, :] == 1) & (before.T[:, None, :] == slot_iota[None, :, None])
    placer = jnp.pad(onehot.astype(bf16), ((0, 0), (0, 1), (0, 0)))
    slot_gate = jnp.sum(jnp.where(onehot, chosen_gate.T[:, None, :], 0.0), axis=2)
    placer = placer.reshape(group, local_experts, capacity + 1, tok_rows).transpose(0, 2, 1, 3)
    token_of = jnp.sum(jnp.where(onehot, jnp.arange(tok_rows, dtype=jnp.int32)[None, None, :], 0), axis=2)
    token_of = jnp.where(jnp.any(onehot, axis=2), token_of, tok_rows)
    source_row = jnp.concatenate(
        [token_of, tok_rows + 1 + jnp.arange(experts, dtype=jnp.int32)[:, None]], axis=1
    )
    source_row = source_row.reshape(group, local_experts, capacity + 1).transpose(0, 2, 1)
    sources = jnp.concatenate(
        [tokens, jnp.zeros((1, model_width), bf16), pack_row(slot_gate, model_width)], axis=0
    )
    outgoing = jnp.take(sources, source_row, axis=0, mode="clip")

    arrived = lax.all_to_all(outgoing, "expert", split_axis=0, concat_axis=0, tiled=True)
    rows_in = arrived
    gates = jnp.swapaxes(join3(arrived[:, capacity, :, :], capacity), 1, 2)
    gates = jnp.pad(gates, ((0, 0), (0, 1), (0, 0)))
    pre_gate = jnp.einsum("sced,edf->scef", rows_in, gate_full, preferred_element_type=f32)
    pre_up = jnp.einsum("sced,edf->scef", rows_in, up_full, preferred_element_type=f32)
    activated, derivative = silu_parts(pre_gate)
    hidden = (activated * pre_up).astype(bf16)
    expert_out = jnp.einsum("scef,efd->sced", hidden, down_full, preferred_element_type=f32).astype(
        bf16
    )
    out_f32 = expert_out.astype(f32)
    partial = jnp.sum(gates[..., None] * out_f32, axis=(1, 2))

    token_mean = jnp.mean(tokens.astype(f32), axis=0)
    shares = lax.all_to_all(partial / tok_rows, "expert", split_axis=0, concat_axis=0, tiled=True)
    own_pooled = token_mean + jnp.sum(shares, axis=0)
    copies = jnp.broadcast_to(own_pooled[None, :], (group, model_width))
    pooled = lax.all_to_all(copies, "expert", split_axis=0, concat_axis=0, tiled=True)
    inv_rms = lax.rsqrt(jnp.mean(pooled * pooled, axis=1) + 1e-06)
    embedding = (pooled * inv_rms[:, None]).astype(bf16)
    blocks = lax.axis_size("dp")
    spread = jnp.broadcast_to(embedding[None], (blocks, group, model_width))
    gathered = lax.all_to_all(spread, "dp", split_axis=0, concat_axis=0, tiled=True)
    gathered = gathered.reshape(blocks * group, model_width)
    batch_size = gathered.shape[0]

    scores = (
        score_scale
        / model_width
        * lax.dot_general(
            gathered, gathered, (((1,), (1,)), ((), ())), preferred_element_type=f32
        )
    )
    batch_iota = jnp.arange(batch_size, dtype=jnp.int32)
    others = batch_iota[:, None] != batch_iota[None, :]
    log_total = jnp.log(jnp.sum(jnp.where(others, jnp.exp(scores), 0.0), axis=1))
    partner_hit = batch_iota[None, :] == partner[:, None]
    partner_score = jnp.sum(jnp.where(partner_hit, scores, 0.0), axis=1)
    contrast_loss = jnp.mean(log_total - partner_score)

    first = row_block * group
    rows = first + jnp.arange(group, dtype=jnp.int32)
    row_scores = lax.dynamic_slice_in_dim(scores, first, group, axis=0)
    row_totals = lax.dynamic_slice_in_dim(log_total, first, group, axis=0)
    row_partner = lax.dynamic_slice_in_dim(partner, first, group, axis=0)
    row_others = rows[:, None] != batch_iota[None, :]
    row_weight = jnp.where(row_others, jnp.exp(row_scores - row_totals[:, None]), 0.0) - (
        batch_iota[None, :] == row_partner[:, None]
    ).astype(f32)
    col_weight = jnp.where(row_others, jnp.exp(row_scores - log_total[None, :]), 0.0) - (
        rows[:, None] == partner[None, :]
    ).astype(f32)
    embed_grad = (
        score_scale
        / model_width
        * jnp.dot(row_weight + col_weight, gathered.astype(f32), precision=highest)
    )
    seq_grad = (
        inv_rms[:, None] * embed_grad
        - (inv_rms**3 * jnp.sum(pooled * embed_grad, axis=1) / model_width)[:, None] * pooled
    )

    slot_dots = jnp.sum(out_f32 * seq_grad[:, None, None, :], axis=3)
    out_grad = (gates[..., None] * seq_grad[:, None, None, :]).astype(bf16)
    hidden_grad = jnp.einsum("sced,efd->scef", out_grad, down_full, preferred_element_type=f32)
    gate_side = (hidden_grad * pre_up * derivative).astype(bf16)
    up_side = (hidden_grad * activated).astype(bf16)
    route_here = jnp.einsum("scef,edf->sced", gate_side, gate_full, preferred_element_type=f32)
    route_here = (
        route_here
        + jnp.einsum("scef,edf->sced", up_side, up_full, preferred_element_type=f32)
    ).astype(bf16)
    grad_row = pack_row(jnp.swapaxes(slot_dots[:, :capacity, :], 1, 2), model_width)
    route_here = route_here.at[:, capacity, :, :].set(grad_row)
    returned = lax.all_to_all(route_here, "expert", split_axis=0, concat_axis=0, tiled=True)

    slot_grads = join3(returned[:, capacity, :, :], capacity).reshape(experts, capacity)
    token_slot_grads = jnp.sum(jnp.where(onehot, slot_grads[:, :, None], 0.0), axis=1).T
    gate_grad = jnp.sum(jnp.where(matches, token_slot_grads[:, None, :], 0.0), axis=2)
    route_sum = jnp.einsum("jcet,jced->td", placer, returned, preferred_element_type=f32)
    own_grad = lax.dynamic_index_in_dim(seq_grad, me, axis=0, keepdims=False)
    token_grad = (own_grad[None, :] + route_sum).astype(bf16)
    return (contrast_loss, token_grad, gate_grad)


def solution(mesh):
    placed = (
        P(("dp", "expert"), None),
        P(("dp", "expert"), None),
        P(("dp", "expert"), None),
        P("expert", "dp", None),
        P("expert", "dp", None),
        P("expert", "dp", None),
        P(),
    )
    return jax.shard_map(
        on_device,
        mesh=mesh,
        in_specs=placed,
        out_specs=(P(), P(("dp", "expert"), None), P(("dp", "expert"), None)),
        check_vma=False,
    )
```

```python
import jax
import jax.numpy as jnp
from jax import lax
from jax.sharding import PartitionSpec as P

score_scale = 20.0
highest = lax.Precision.HIGHEST
f32 = jnp.float32
bf16 = jnp.bfloat16


def silu_parts(pre_act):
    sigmoid_val = jax.nn.sigmoid(pre_act)
    return (pre_act * sigmoid_val, sigmoid_val * (1.0 + pre_act * (1.0 - sigmoid_val)))


def split3(x):
    hi = lax.reduce_precision(x, exponent_bits=8, mantissa_bits=7)
    rest = x - hi
    mid = lax.reduce_precision(rest, exponent_bits=8, mantissa_bits=7)
    lo = rest - mid
    return jnp.concatenate([hi, mid, lo], axis=-1).astype(bf16)


def join3(packed, n):
    hi = packed[..., :n].astype(f32)
    mid = packed[..., n : 2 * n].astype(f32)
    lo = packed[..., 2 * n : 3 * n].astype(f32)
    return hi + (mid + lo)


def pack_row(values, width):
    pieces = split3(values)
    pad = width - pieces.shape[-1]
    return jnp.pad(pieces, [(0, 0)] * (pieces.ndim - 1) + [(0, pad)])


def on_device(tokens, expert_ids, gate_values, w_gate, w_up, w_down, partner):
    tok_rows, model_width = tokens.shape
    route_count = expert_ids.shape[1]
    local_experts = w_gate.shape[0]
    group = lax.axis_size("expert")
    experts = group * local_experts
    capacity = tok_rows * route_count // experts + max(1, tok_rows * route_count // (16 * experts))
    slot_total = experts * capacity
    me = lax.axis_index("expert")
    row_block = lax.axis_index(("z", "core"))

    ff_width = w_gate.shape[2]
    stacked = jnp.stack([w_gate, w_up, w_down.reshape(w_gate.shape)])
    every = lax.all_gather(stacked, ("z", "core"), axis=2, tiled=True)
    gate_full = every[0]
    up_full = every[1]
    down_full = every[2].reshape(local_experts, ff_width, model_width)

    expert_iota = jnp.arange(experts, dtype=jnp.int32)
    matches = expert_ids[:, :, None] == expert_iota
    chosen = jnp.sum(matches.astype(jnp.int32), axis=1, dtype=jnp.int32)
    chosen_gate = jnp.sum(jnp.where(matches, gate_values[:, :, None], 0.0), axis=1)
    before = jnp.cumsum(chosen, axis=0, dtype=jnp.int32) - chosen
    slot_rank = jnp.sum(jnp.where(matches, before[:, None, :], 0), axis=2, dtype=jnp.int32)
    slot_iota = jnp.arange(capacity, dtype=jnp.int32)
    onehot = (chosen.T[:, None, :] == 1) & (before.T[:, None, :] == slot_iota[None, :, None])
    placer = jnp.pad(onehot.astype(bf16), ((0, 0), (0, 1), (0, 0)))
    slot_gate = jnp.sum(jnp.where(onehot, chosen_gate.T[:, None, :], 0.0), axis=2)
    placer = placer.reshape(group, local_experts, capacity + 1, tok_rows).transpose(0, 2, 1, 3)
    outgoing = jnp.einsum("jcet,td->jced", placer, tokens, preferred_element_type=f32).astype(bf16)
    gate_row = pack_row(slot_gate, model_width).reshape(group, local_experts, model_width)
    outgoing = outgoing.at[:, capacity, :, :].set(gate_row)

    arrived = lax.all_to_all(outgoing, "expert", split_axis=0, concat_axis=0, tiled=True)
    rows_in = arrived
    gates = jnp.swapaxes(join3(arrived[:, capacity, :, :], capacity), 1, 2)
    gates = jnp.pad(gates, ((0, 0), (0, 1), (0, 0)))
    pre_gate = jnp.einsum("sced,edf->scef", rows_in, gate_full, preferred_element_type=f32)
    pre_up = jnp.einsum("sced,edf->scef", rows_in, up_full, preferred_element_type=f32)
    activated, derivative = silu_parts(pre_gate)
    hidden = (activated * pre_up).astype(bf16)
    expert_out = jnp.einsum("scef,efd->sced", hidden, down_full, preferred_element_type=f32).astype(
        bf16
    )
    out_f32 = expert_out.astype(f32)
    partial = jnp.sum(gates[..., None] * out_f32, axis=(1, 2))

    token_mean = jnp.mean(tokens.astype(f32), axis=0)
    shares = lax.all_to_all(partial / tok_rows, "expert", split_axis=0, concat_axis=0, tiled=True)
    own_pooled = token_mean + jnp.sum(shares, axis=0)
    copies = jnp.broadcast_to(own_pooled[None, :], (group, model_width))
    pooled = lax.all_to_all(copies, "expert", split_axis=0, concat_axis=0, tiled=True)
    inv_rms = lax.rsqrt(jnp.mean(pooled * pooled, axis=1) + 1e-06)
    embedding = (pooled * inv_rms[:, None]).astype(bf16)
    chips = lax.axis_size("z")
    cores = lax.axis_size("core")
    spread = jnp.broadcast_to(embedding[None], (chips, group, model_width))
    along_z = lax.all_to_all(spread, "z", split_axis=0, concat_axis=0, tiled=True)
    pair = jnp.broadcast_to(along_z[None], (cores,) + along_z.shape)
    both = lax.all_to_all(pair, "core", split_axis=0, concat_axis=0, tiled=True)
    gathered = jnp.swapaxes(both, 0, 1).reshape(chips * cores * group, model_width)
    blocks = chips * cores
    batch_size = gathered.shape[0]

    scores = (
        score_scale
        / model_width
        * lax.dot_general(
            gathered, gathered, (((1,), (1,)), ((), ())), preferred_element_type=f32
        )
    )
    batch_iota = jnp.arange(batch_size, dtype=jnp.int32)
    others = batch_iota[:, None] != batch_iota[None, :]
    log_total = jnp.log(jnp.sum(jnp.where(others, jnp.exp(scores), 0.0), axis=1))
    partner_hit = batch_iota[None, :] == partner[:, None]
    partner_score = jnp.sum(jnp.where(partner_hit, scores, 0.0), axis=1)
    contrast_loss = jnp.mean(log_total - partner_score)

    first = row_block * group
    rows = first + jnp.arange(group, dtype=jnp.int32)
    row_scores = lax.dynamic_slice_in_dim(scores, first, group, axis=0)
    row_totals = lax.dynamic_slice_in_dim(log_total, first, group, axis=0)
    row_partner = lax.dynamic_slice_in_dim(partner, first, group, axis=0)
    row_others = rows[:, None] != batch_iota[None, :]
    row_weight = jnp.where(row_others, jnp.exp(row_scores - row_totals[:, None]), 0.0) - (
        batch_iota[None, :] == row_partner[:, None]
    ).astype(f32)
    col_weight = jnp.where(row_others, jnp.exp(row_scores - log_total[None, :]), 0.0) - (
        rows[:, None] == partner[None, :]
    ).astype(f32)
    embed_grad = (
        score_scale
        / model_width
        * jnp.dot(row_weight + col_weight, gathered.astype(f32), precision=highest)
    )
    seq_grad = (
        inv_rms[:, None] * embed_grad
        - (inv_rms**3 * jnp.sum(pooled * embed_grad, axis=1) / model_width)[:, None] * pooled
    )

    slot_dots = jnp.sum(out_f32 * seq_grad[:, None, None, :], axis=3)
    out_grad = (gates[..., None] * seq_grad[:, None, None, :]).astype(bf16)
    hidden_grad = jnp.einsum("sced,efd->scef", out_grad, down_full, preferred_element_type=f32)
    gate_side = (hidden_grad * pre_up * derivative).astype(bf16)
    up_side = (hidden_grad * activated).astype(bf16)
    route_here = jnp.einsum("scef,edf->sced", gate_side, gate_full, preferred_element_type=f32)
    route_here = (
        route_here
        + jnp.einsum("scef,edf->sced", up_side, up_full, preferred_element_type=f32)
    ).astype(bf16)
    grad_row = pack_row(jnp.swapaxes(slot_dots[:, :capacity, :], 1, 2), model_width)
    route_here = route_here.at[:, capacity, :, :].set(grad_row)
    returned = lax.all_to_all(route_here, "expert", split_axis=0, concat_axis=0, tiled=True)

    slot_grads = join3(returned[:, capacity, :, :], capacity).reshape(experts, capacity)
    token_slot_grads = jnp.sum(jnp.where(onehot, slot_grads[:, :, None], 0.0), axis=1).T
    gate_grad = jnp.sum(jnp.where(matches, token_slot_grads[:, None, :], 0.0), axis=2)
    route_sum = jnp.einsum("jcet,jced->td", placer, returned, preferred_element_type=f32)
    own_grad = lax.dynamic_index_in_dim(seq_grad, me, axis=0, keepdims=False)
    token_grad = (own_grad[None, :] + route_sum).astype(bf16)
    return (contrast_loss, token_grad, gate_grad)


def solution(mesh):
    chips_z = mesh.shape["dp"] // 2
    split_mesh = jax.sharding.Mesh(
        mesh.devices.reshape(chips_z, 2, mesh.shape["expert"]), ("z", "core", "expert")
    )
    rows = ("z", "core", "expert")
    placed = (
        P(rows, None),
        P(rows, None),
        P(rows, None),
        P("expert", ("z", "core"), None),
        P("expert", ("z", "core"), None),
        P("expert", ("z", "core"), None),
        P(),
    )
    return jax.shard_map(
        on_device,
        mesh=split_mesh,
        in_specs=placed,
        out_specs=(P(), P(rows, None), P(rows, None)),
        check_vma=False,
    )
```

```python
import jax
import jax.numpy as jnp
from jax import lax
from jax.sharding import PartitionSpec as P

score_scale = 20.0
highest = lax.Precision.HIGHEST
f32 = jnp.float32
bf16 = jnp.bfloat16


def silu_parts(pre_act):
    sigmoid_val = jax.nn.sigmoid(pre_act)
    return (pre_act * sigmoid_val, sigmoid_val * (1.0 + pre_act * (1.0 - sigmoid_val)))


def split3(x):
    hi = lax.reduce_precision(x, exponent_bits=8, mantissa_bits=7)
    rest = x - hi
    mid = lax.reduce_precision(rest, exponent_bits=8, mantissa_bits=7)
    lo = rest - mid
    return jnp.concatenate([hi, mid, lo], axis=-1).astype(bf16)


def join3(packed, n):
    hi = packed[..., :n].astype(f32)
    mid = packed[..., n : 2 * n].astype(f32)
    lo = packed[..., 2 * n : 3 * n].astype(f32)
    return hi + (mid + lo)


def pack_row(values, width):
    pieces = split3(values)
    pad = width - pieces.shape[-1]
    return jnp.pad(pieces, [(0, 0)] * (pieces.ndim - 1) + [(0, pad)])


def on_device(tokens, expert_ids, gate_values, w_gate, w_up, w_down, partner):
    tok_rows, model_width = tokens.shape
    route_count = expert_ids.shape[1]
    local_experts = w_gate.shape[0]
    group = lax.axis_size("expert")
    experts = group * local_experts
    capacity = tok_rows * route_count // experts + max(1, tok_rows * route_count // (16 * experts))
    slot_total = experts * capacity
    me = lax.axis_index("expert")
    row_block = lax.axis_index(("z", "core"))

    ff_width = w_gate.shape[2]
    stacked = jnp.stack([w_gate, w_up, w_down.reshape(w_gate.shape)])
    every = lax.all_gather(stacked, ("z", "core"), axis=2, tiled=True)
    gate_full = every[0]
    up_full = every[1]
    down_full = every[2].reshape(local_experts, ff_width, model_width)

    expert_iota = jnp.arange(experts, dtype=jnp.int32)
    matches = expert_ids[:, :, None] == expert_iota
    chosen = jnp.sum(matches.astype(jnp.int32), axis=1, dtype=jnp.int32)
    chosen_gate = jnp.sum(jnp.where(matches, gate_values[:, :, None], 0.0), axis=1)
    before = jnp.cumsum(chosen, axis=0, dtype=jnp.int32) - chosen
    slot_rank = jnp.sum(jnp.where(matches, before[:, None, :], 0), axis=2, dtype=jnp.int32)
    slot_iota = jnp.arange(capacity, dtype=jnp.int32)
    onehot = (chosen.T[:, None, :] == 1) & (before.T[:, None, :] == slot_iota[None, :, None])
    placer = jnp.pad(onehot.astype(bf16), ((0, 0), (0, 1), (0, 0)))
    slot_gate = jnp.sum(jnp.where(onehot, chosen_gate.T[:, None, :], 0.0), axis=2)
    placer = placer.reshape(group, local_experts, capacity + 1, tok_rows).transpose(0, 2, 1, 3)
    outgoing = jnp.einsum("jcet,td->jced", placer, tokens, preferred_element_type=f32).astype(bf16)
    gate_row = pack_row(slot_gate, model_width).reshape(group, local_experts, model_width)
    outgoing = outgoing.at[:, capacity, :, :].set(gate_row)

    arrived = lax.all_to_all(outgoing, "expert", split_axis=0, concat_axis=0, tiled=True)
    rows_in = arrived
    gates = jnp.swapaxes(join3(arrived[:, capacity, :, :], capacity), 1, 2)
    gates = jnp.pad(gates, ((0, 0), (0, 1), (0, 0)))
    pre_gate = jnp.einsum("sced,edf->scef", rows_in, gate_full, preferred_element_type=f32)
    pre_up = jnp.einsum("sced,edf->scef", rows_in, up_full, preferred_element_type=f32)
    activated, derivative = silu_parts(pre_gate)
    hidden = (activated * pre_up).astype(bf16)
    expert_out = jnp.einsum("scef,efd->sced", hidden, down_full, preferred_element_type=f32).astype(
        bf16
    )
    out_f32 = expert_out.astype(f32)
    partial = jnp.sum(gates[..., None] * out_f32, axis=(1, 2))

    token_mean = jnp.mean(tokens.astype(f32), axis=0)
    shares = lax.all_to_all(partial / tok_rows, "expert", split_axis=0, concat_axis=0, tiled=True)
    own_pooled = token_mean + jnp.sum(shares, axis=0)
    copies = jnp.broadcast_to(own_pooled[None, :], (group, model_width))
    pooled = lax.all_to_all(copies, "expert", split_axis=0, concat_axis=0, tiled=True)
    inv_rms = lax.rsqrt(jnp.mean(pooled * pooled, axis=1) + 1e-06)
    embedding = (pooled * inv_rms[:, None]).astype(bf16)
    chips = lax.axis_size("z")
    cores = lax.axis_size("core")
    spread = jnp.broadcast_to(embedding[None], (chips, group, model_width))
    along_z = lax.all_to_all(spread, "z", split_axis=0, concat_axis=0, tiled=True)
    sibling = lax.ppermute(along_z, "core", [(c, c ^ 1) for c in range(cores)])
    low_core = lax.axis_index("core") == 0
    both = jnp.where(low_core, jnp.stack([along_z, sibling]), jnp.stack([sibling, along_z]))
    gathered = jnp.swapaxes(both, 0, 1).reshape(chips * cores * group, model_width)
    blocks = chips * cores
    batch_size = gathered.shape[0]

    scores = (
        score_scale
        / model_width
        * lax.dot_general(
            gathered, gathered, (((1,), (1,)), ((), ())), preferred_element_type=f32
        )
    )
    batch_iota = jnp.arange(batch_size, dtype=jnp.int32)
    others = batch_iota[:, None] != batch_iota[None, :]
    log_total = jnp.log(jnp.sum(jnp.where(others, jnp.exp(scores), 0.0), axis=1))
    partner_hit = batch_iota[None, :] == partner[:, None]
    partner_score = jnp.sum(jnp.where(partner_hit, scores, 0.0), axis=1)
    contrast_loss = jnp.mean(log_total - partner_score)

    first = row_block * group
    rows = first + jnp.arange(group, dtype=jnp.int32)
    row_scores = lax.dynamic_slice_in_dim(scores, first, group, axis=0)
    row_totals = lax.dynamic_slice_in_dim(log_total, first, group, axis=0)
    row_partner = lax.dynamic_slice_in_dim(partner, first, group, axis=0)
    row_others = rows[:, None] != batch_iota[None, :]
    row_weight = jnp.where(row_others, jnp.exp(row_scores - row_totals[:, None]), 0.0) - (
        batch_iota[None, :] == row_partner[:, None]
    ).astype(f32)
    col_weight = jnp.where(row_others, jnp.exp(row_scores - log_total[None, :]), 0.0) - (
        rows[:, None] == partner[None, :]
    ).astype(f32)
    embed_grad = (
        score_scale
        / model_width
        * jnp.dot(row_weight + col_weight, gathered.astype(f32), precision=highest)
    )
    seq_grad = (
        inv_rms[:, None] * embed_grad
        - (inv_rms**3 * jnp.sum(pooled * embed_grad, axis=1) / model_width)[:, None] * pooled
    )

    slot_dots = jnp.sum(out_f32 * seq_grad[:, None, None, :], axis=3)
    out_grad = (gates[..., None] * seq_grad[:, None, None, :]).astype(bf16)
    hidden_grad = jnp.einsum("sced,efd->scef", out_grad, down_full, preferred_element_type=f32)
    gate_side = (hidden_grad * pre_up * derivative).astype(bf16)
    up_side = (hidden_grad * activated).astype(bf16)
    route_here = jnp.einsum("scef,edf->sced", gate_side, gate_full, preferred_element_type=f32)
    route_here = (
        route_here
        + jnp.einsum("scef,edf->sced", up_side, up_full, preferred_element_type=f32)
    ).astype(bf16)
    grad_row = pack_row(jnp.swapaxes(slot_dots[:, :capacity, :], 1, 2), model_width)
    route_here = route_here.at[:, capacity, :, :].set(grad_row)
    returned = lax.all_to_all(route_here, "expert", split_axis=0, concat_axis=0, tiled=True)

    slot_grads = join3(returned[:, capacity, :, :], capacity).reshape(experts, capacity)
    token_slot_grads = jnp.sum(jnp.where(onehot, slot_grads[:, :, None], 0.0), axis=1).T
    gate_grad = jnp.sum(jnp.where(matches, token_slot_grads[:, None, :], 0.0), axis=2)
    route_sum = jnp.einsum("jcet,jced->td", placer, returned, preferred_element_type=f32)
    own_grad = lax.dynamic_index_in_dim(seq_grad, me, axis=0, keepdims=False)
    token_grad = (own_grad[None, :] + route_sum).astype(bf16)
    return (contrast_loss, token_grad, gate_grad)


def solution(mesh):
    chips_z = mesh.shape["dp"] // 2
    split_mesh = jax.sharding.Mesh(
        mesh.devices.reshape(chips_z, 2, mesh.shape["expert"]), ("z", "core", "expert")
    )
    rows = ("z", "core", "expert")
    placed = (
        P(rows, None),
        P(rows, None),
        P(rows, None),
        P("expert", ("z", "core"), None),
        P("expert", ("z", "core"), None),
        P("expert", ("z", "core"), None),
        P(),
    )
    return jax.shard_map(
        on_device,
        mesh=split_mesh,
        in_specs=placed,
        out_specs=(P(), P(rows, None), P(rows, None)),
        check_vma=False,
    )
```
